32 devices in a mesh: gx: 8 (over z, y), gy: 4 (over x, core).
Axes of the slice: x: 2, y: 2, z: 4, core: 2. Of those that a mesh axis runs over, the one named last changes fastest.
Arguments:
- volume: bfloat16 [256, 128, 2048], P('gx', 'gy'), may hold values from -60 to 60, as said below
- tissue: int32 [16, 8, 2], P(None, 'gy'), may hold values from 0 to 1, as said below
- w_conv: bfloat16 [3, 3, 3, 64, 128], replicated, may hold values from -0.15625 to 0.15625
- gamma: float32 [128], replicated, may hold values from 0.5 to 1.5
- beta: float32 [128], replicated, may hold values from -3 to 3
- w_down: bfloat16 [2, 2, 2, 128, 128], replicated, may hold values from -0.1875 to 0.1875
- b_down: float32 [128], replicated, may hold values from -3 to 3
Outputs:
- features: bfloat16 [128, 64, 2048], P('gx', 'gy')
The draws below stay inside these ranges and needn't reach their ends.
Inputs may be any that keep to these rules, and one draw needn't show every extreme that they name: In every draw some device's 4 * 2 tiles all have tissue = 1; the tiles with tissue differ in number from device to device. `volume`: voxel and channel scales vary.
All inputs are finite; a program needn't handle non-finite values.
Results may differ from the reference program's by a relative error of at most 0.0046.
Values may be sent and summed in bfloat16 or wider, within the bound.
No kernel may reach another device: no remote copies, remote signals or barrier semaphores. Data moves between devices by JAX's collectives and lax.ppermute only.
A program may use at most 128 MiB of HBM per device.

```python
import math
import jax
import jax.numpy as jnp
from jax import lax

CIN = 64
CMID = 128
COUT = 128
GROUPS = 8
TILE = 16
TZ = 2
NTX = 16
NTY = 8
NX = 256
NY = 128
NZ = 32


def draw_volume(key, part):
    key_base = jax.random.fold_in(key, 11)
    key_chan = jax.random.fold_in(key, 12)
    key_voxel = jax.random.fold_in(key, 13)
    shape_full = (NX, NY, NZ, CIN)
    base = jnp.clip(jax.random.normal(key_base, shape_full, jnp.float32), -6.0, 6.0)
    chan_scale = jnp.exp(jax.random.uniform(key_chan, (CIN,), jnp.float32, math.log(0.3), math.log(3.0)))
    voxel_scale = jnp.exp(jax.random.uniform(key_voxel, (NX, NY, NZ, 1), jnp.float32, math.log(0.3), math.log(3.0)))
    values = base * chan_scale * voxel_scale
    return values.reshape(NX, NY, NZ * CIN).astype(jnp.bfloat16)


def draw_tissue(key, part):
    key_level = jax.random.fold_in(key, 21)
    key_fullx = jax.random.fold_in(key, 22)
    key_fully = jax.random.fold_in(key, 23)
    key_score = jax.random.fold_in(key, 24)
    blocks_x = NTX // 2
    blocks_y = NTY // 2
    tiles_dev = 4 * TZ
    levels = jax.random.randint(key_level, (blocks_x, blocks_y), 0, tiles_dev + 1)
    full_x = jax.random.randint(key_fullx, (), 0, blocks_x)
    full_y = jax.random.randint(key_fully, (), 0, blocks_y)
    chosen = (jnp.arange(blocks_x)[:, None] == full_x) & (jnp.arange(blocks_y)[None, :] == full_y)
    levels = jnp.where(chosen, tiles_dev, levels)
    scores = jax.random.randint(key_score, (blocks_x, blocks_y, tiles_dev), 0, 1 << 20) * tiles_dev
    scores = scores + jnp.arange(tiles_dev, dtype=jnp.int32)
    ranking = jnp.argsort(jnp.argsort(scores, axis=-1), axis=-1)
    occupied = (ranking < levels[:, :, None]).astype(jnp.int32)
    occupied = occupied.reshape(blocks_x, blocks_y, 2, 2, TZ).transpose(0, 2, 1, 3, 4)
    return occupied.reshape(NTX, NTY, TZ)


def scatter_about(key, shape, scale, most, kind=jnp.bfloat16):
    return jnp.clip(scale * jax.random.normal(key, shape, jnp.float32), -most, most).astype(kind)


def setup_inputs(seed: int = 0) -> dict:
    splits = jax.random.split(jax.random.key(seed), 8)
    volume = draw_volume(jax.random.fold_in(splits[7], 71), 0)
    tissue = draw_tissue(jax.random.fold_in(splits[7], 71), 0)
    w_conv = scatter_about(splits[2], (3, 3, 3, CIN, CMID), (27 * CIN) ** -0.5, 0.15625)
    gamma = jnp.clip(jax.random.uniform(splits[3], (CMID,), jnp.float32, 0.5, 1.5), 0.5, 1.5)
    beta = scatter_about(splits[4], (CMID,), 0.5, 3.0, jnp.float32)
    w_down = scatter_about(splits[5], (2, 2, 2, CMID, COUT), (8 * CMID) ** -0.5, 0.1875)
    b_down = scatter_about(splits[6], (COUT,), 0.5, 3.0, jnp.float32)
    return dict(volume=volume, tissue=tissue, w_conv=w_conv, gamma=gamma, beta=beta, w_down=w_down, b_down=b_down)


def tile_features(window, w_conv, gamma, beta, w_down, b_down):
    side_cells = window.shape[0] - 2
    in_channels = window.shape[3]
    summed = jnp.zeros((side_cells ** 3, w_conv.shape[4]), jnp.float32)
    for tap_index in range(27):
        shift_x = tap_index // 9
        shift_y = tap_index // 3 % 3
        shift_z = tap_index % 3
        shifted = window[shift_x:shift_x + side_cells, shift_y:shift_y + side_cells, shift_z:shift_z + side_cells, :]
        shifted = shifted.reshape(side_cells ** 3, in_channels)
        summed = summed + jnp.dot(shifted, w_conv[shift_x, shift_y, shift_z], preferred_element_type=jnp.float32)
    grouped = summed.reshape(side_cells ** 3, GROUPS, -1)
    group_mean = lax.optimization_barrier(jnp.mean(grouped, axis=(0, 2), keepdims=True))
    group_var = lax.optimization_barrier(jnp.mean(jnp.square(grouped - group_mean), axis=(0, 2), keepdims=True))
    normed = ((grouped - group_mean) * lax.rsqrt(group_var + 1e-05)).reshape(side_cells ** 3, -1)
    active = jnp.maximum(normed * gamma + beta, 0.0).astype(jnp.bfloat16)
    half_side = side_cells // 2
    blocks = active.reshape(half_side, 2, half_side, 2, half_side, 2, -1)
    pooled = jnp.zeros((half_side ** 3, w_down.shape[4]), jnp.float32) + b_down
    for corner_index in range(8):
        pick_a = corner_index // 4
        pick_b = corner_index // 2 % 2
        pick_c = corner_index % 2
        corner = blocks[:, pick_a, :, pick_b, :, pick_c, :].reshape(half_side ** 3, -1)
        pooled = pooled + jnp.dot(corner, w_down[pick_a, pick_b, pick_c], preferred_element_type=jnp.float32)
    return pooled.astype(jnp.bfloat16).reshape(half_side, half_side, half_side, -1)

def reference(volume, tissue, w_conv, gamma, beta, w_down, b_down):
    voxels = volume.reshape(NX, NY, NZ, CIN)
    padded = jnp.pad(voxels, ((1, 1), (1, 1), (1, 1), (0, 0)))
    tile_total = NTX * NTY * TZ
    half_side = TILE // 2

    def tile_output(flat_index):
        tile_x = flat_index // (NTY * TZ)
        tile_y = flat_index // TZ % NTY
        tile_z = flat_index % TZ
        window = lax.dynamic_slice(padded, (tile_x * TILE, tile_y * TILE, tile_z * TILE, 0 * tile_x), (TILE + 2, TILE + 2, TILE + 2, CIN))
        occupied = tissue[tile_x, tile_y, tile_z]
        return lax.cond(occupied > 0, lambda window_in: tile_features(window_in, w_conv, gamma, beta, w_down, b_down), lambda window_in: jnp.zeros((half_side, half_side, half_side, COUT), jnp.bfloat16), window)
    tile_stack = lax.map(tile_output, jnp.arange(tile_total, dtype=jnp.int32))
    tile_stack = tile_stack.reshape(NTX, NTY, TZ, half_side, half_side, half_side, COUT)
    tile_stack = tile_stack.transpose(0, 3, 1, 4, 2, 5, 6)
    return tile_stack.reshape(NX // 2, NY // 2, NZ // 2 * COUT)
```

```python
import jax
import jax.numpy as jnp
from jax import lax
from jax.experimental import pallas as pl
from jax.experimental.pallas import tpu as pltpu
from jax.sharding import PartitionSpec as P

CIN = 64
CMID = 128
COUT = 128
GROUPS = 8
TILE = 16
EPS = 1e-05


def with_halo(block, sides, width):
    for axis, dim in sides:
        count = lax.axis_size(axis)
        forward = [(i, i + 1) for i in range(count - 1)]
        backward = [(target, source) for source, target in forward]
        low = lax.ppermute(
            lax.slice_in_dim(block, block.shape[dim] - width, None, axis=dim), axis, forward
        )
        high = lax.ppermute(lax.slice_in_dim(block, 0, width, axis=dim), axis, backward)
        block = jnp.concatenate([low, block, high], axis=dim)
    return block


def build_band(w_conv):
    in_pos = jnp.arange(4, dtype=jnp.int32)[:, None, None]
    out_pos = jnp.arange(2, dtype=jnp.int32)[None, :, None]
    taps = jnp.arange(3, dtype=jnp.int32)[None, None, :]
    select = (in_pos - out_pos == taps).astype(jnp.float32)
    band = jnp.einsum("zod,xydcm->xyzcom", select, w_conv.astype(jnp.float32))
    return band.reshape(9, 4 * CIN, 2 * CMID).astype(jnp.bfloat16)


def group_sum(row, indicator):
    row = jnp.broadcast_to(row, (8, row.shape[1]))
    total = jnp.zeros(row.shape, jnp.float32)
    rest = row
    for _ in range(3):
        piece = rest.astype(jnp.bfloat16)
        total = total + jnp.dot(piece, indicator, preferred_element_type=jnp.float32)
        rest = rest - piece.astype(jnp.float32)
    return total[0:1]


def tile_kernel(flags_ref, win_ref, band_ref, ind_ref, gamma_ref, beta_ref, down_ref,
                bias_ref, out_ref, conv_ref):
    tile = pl.program_id(0)
    rows = TILE * TILE
    pairs = TILE // 2
    half = TILE // 2

    @pl.when(flags_ref[tile] > 0)
    def _():
        for pair in range(pairs):
            acc = None
            for tap in range(9):
                shift_x, shift_y = tap // 3, tap % 3
                slab = win_ref[0, shift_y, shift_x:shift_x + TILE, :,
                               2 * CIN * pair:2 * CIN * pair + 4 * CIN]
                part = jnp.dot(slab.reshape(rows, 4 * CIN), band_ref[tap],
                               preferred_element_type=jnp.float32)
                acc = part if acc is None else acc + part
            conv_ref[2 * pair] = acc[:, :CMID]
            conv_ref[2 * pair + 1] = acc[:, CMID:]

        count = float(rows * TILE * (CMID // GROUPS))
        indicator = ind_ref[...]
        total = jnp.zeros((1, CMID), jnp.float32)
        for depth in range(TILE):
            total = total + jnp.sum(conv_ref[depth], axis=0, keepdims=True)
        mean = group_sum(total, indicator) / count
        total = jnp.zeros((1, CMID), jnp.float32)
        for depth in range(TILE):
            diff = conv_ref[depth] - mean
            total = total + jnp.sum(diff * diff, axis=0, keepdims=True)
        var = group_sum(total, indicator) / count
        scale = lax.rsqrt(var + EPS) * gamma_ref[...]
        shift = beta_ref[...]
        for depth in range(TILE):
            conv_ref[depth] = jnp.maximum((conv_ref[depth] - mean) * scale + shift, 0.0)

        results = [jnp.zeros((half * half, COUT), jnp.float32) for _ in range(half)]
        for pick_b in range(2):
            picked = conv_ref[:, pl.ds(pick_b, rows // 2, stride=2), :]
            for pick_a in range(2):
                corners = [
                    picked[depth].reshape(half, 2, half, CMID)[:, pick_a]
                    .reshape(half * half, CMID).astype(jnp.bfloat16)
                    for depth in range(TILE)
                ]
                weight = down_ref[pick_a * 2 + pick_b]
                for depth in range(half):
                    lhs = jnp.concatenate([corners[2 * depth], corners[2 * depth + 1]], axis=1)
                    results[depth] = results[depth] + jnp.dot(
                        lhs, weight, preferred_element_type=jnp.float32)
        bias = bias_ref[...]
        out_ref[0] = jnp.concatenate([r + bias for r in results], axis=1).astype(jnp.bfloat16)

    @pl.when(flags_ref[tile] == 0)
    def _():
        out_ref[...] = jnp.zeros(out_ref.shape, out_ref.dtype)


def shards(volume, tissue, w_conv, gamma, beta, w_down, b_down):
    own_index = lax.axis_index("gx")
    size_x, size_y, merged = volume.shape
    size_z = merged // CIN
    tiles_x, tiles_y, tiles_z = size_x // TILE, size_y // TILE, size_z // TILE
    tile_count = tiles_x * tiles_y * tiles_z
    half = TILE // 2
    grown = with_halo(volume, (("gx", 0), ("gy", 1)), 1)
    grown = jnp.pad(grown, ((0, 0), (0, 0), (CIN, CIN)))
    depth_lanes = (TILE + 2) * CIN
    windows = []
    for i in range(tiles_x):
        for j in range(tiles_y):
            for k in range(tiles_z):
                shifted = [
                    grown[TILE * i:TILE * i + TILE + 2, TILE * j + dy:TILE * j + dy + TILE,
                          TILE * CIN * k:TILE * CIN * k + depth_lanes]
                    for dy in range(3)
                ]
                windows.append(jnp.stack(shifted))
    windows = jnp.stack(windows)
    band = build_band(w_conv)
    lane = jnp.arange(CMID, dtype=jnp.int32)
    group_size = CMID // GROUPS
    indicator = (lane[:, None] // group_size == lane[None, :] // group_size).astype(jnp.bfloat16)
    down = w_down.reshape(4, 2 * CMID, COUT)
    own_tissue = lax.dynamic_slice_in_dim(tissue, own_index * tiles_x, tiles_x, 0)
    flags = own_tissue.reshape(tile_count).astype(jnp.int32)

    full = lambda shape: pl.BlockSpec(shape, lambda t, f: (0,) * len(shape))
    grid_spec = pltpu.PrefetchScalarGridSpec(
        num_scalar_prefetch=1,
        grid=(tile_count,),
        in_specs=[
            pl.BlockSpec((1, 3, TILE + 2, TILE, depth_lanes), lambda t, f: (t, 0, 0, 0, 0)),
            full((9, 4 * CIN, 2 * CMID)),
            full((CMID, CMID)),
            full((1, CMID)),
            full((1, CMID)),
            full((4, 2 * CMID, COUT)),
            full((1, COUT)),
        ],
        out_specs=pl.BlockSpec((1, half * half, half * COUT), lambda t, f: (t, 0, 0)),
        scratch_shapes=[pltpu.VMEM((TILE, TILE * TILE, CMID), jnp.float32)],
    )
    result = pl.pallas_call(
        tile_kernel,
        grid_spec=grid_spec,
        out_shape=jax.ShapeDtypeStruct((tile_count, half * half, half * COUT), jnp.bfloat16),
    )(
        flags,
        windows,
        band,
        indicator,
        gamma.reshape(1, CMID),
        beta.reshape(1, CMID),
        down,
        b_down.reshape(1, COUT),
    )
    result = result.reshape(tiles_x, tiles_y, tiles_z, half, half, half * COUT)
    result = result.transpose(0, 3, 1, 4, 2, 5)
    return result.reshape(size_x // 2, size_y // 2, size_z // 2 * COUT)


def solution(mesh):
    in_specs = (P("gx", "gy", None), P(None, "gy", None), P(), P(), P(), P(), P())
    out_specs = P("gx", "gy", None)
    return jax.shard_map(shards, mesh=mesh, in_specs=in_specs, out_specs=out_specs, check_vma=False)
```

```python
import jax
import jax.numpy as jnp
from jax import lax
from jax.experimental import pallas as pl
from jax.experimental.pallas import tpu as pltpu
from jax.sharding import PartitionSpec as P

CIN = 64
CMID = 128
COUT = 128
GROUPS = 8
TILE = 16
EPS = 1e-05


def with_halo(block, sides, width):
    for axis, dim in sides:
        count = lax.axis_size(axis)
        forward = [(i, i + 1) for i in range(count - 1)]
        backward = [(target, source) for source, target in forward]
        low = lax.ppermute(
            lax.slice_in_dim(block, block.shape[dim] - width, None, axis=dim), axis, forward
        )
        high = lax.ppermute(lax.slice_in_dim(block, 0, width, axis=dim), axis, backward)
        block = jnp.concatenate([low, block, high], axis=dim)
    return block


def build_band(w_conv):
    in_pos = jnp.arange(4, dtype=jnp.int32)[:, None, None]
    out_pos = jnp.arange(2, dtype=jnp.int32)[None, :, None]
    taps = jnp.arange(3, dtype=jnp.int32)[None, None, :]
    select = (in_pos - out_pos == taps).astype(jnp.float32)
    band = jnp.einsum("zod,xydcm->xyzcom", select, w_conv.astype(jnp.float32))
    return band.reshape(9, 4 * CIN, 2 * CMID).astype(jnp.bfloat16)


def group_sum(row, indicator):
    row = jnp.broadcast_to(row, (8, row.shape[1]))
    total = jnp.zeros(row.shape, jnp.float32)
    rest = row
    for _ in range(3):
        piece = rest.astype(jnp.bfloat16)
        total = total + jnp.dot(piece, indicator, preferred_element_type=jnp.float32)
        rest = rest - piece.astype(jnp.float32)
    return total[0:1]


def tile_kernel(flags_ref, grown_ref, band_ref, ind_ref, gamma_ref, beta_ref, down_ref,
                bias_ref, out_ref, win_ref, conv_ref):
    pos_x, pos_y, pos_z = pl.program_id(0), pl.program_id(1), pl.program_id(2)
    tiles_y, tiles_z = pl.num_programs(1), pl.num_programs(2)
    flag = flags_ref[(pos_x * tiles_y + pos_y) * tiles_z + pos_z]
    rows = TILE * TILE
    half = TILE // 2
    pairs = half + 1
    span = TILE * CIN
    pad = 2 * CIN
    lanes = span + 2 * pad
    rows_x = pl.ds(pos_x * TILE, TILE + 2)
    start = pl.multiple_of(pos_z * span, 128)

    @pl.when(flag > 0)
    def _():
        for col in range(grown_ref.shape[1] // TILE):
            @pl.when(pos_y == col)
            def _():
                for shift_y in range(3):
                    rows_y = pl.ds(col * TILE + shift_y, TILE)
                    win_ref[shift_y, :, :, pad:pad + span] = grown_ref[rows_x, rows_y,
                                                                       pl.ds(start, span)]
                    below = grown_ref[rows_x, rows_y, pl.ds(pl.multiple_of(jnp.maximum(start - pad, 0), 128), pad)]
                    win_ref[shift_y, :, :, 0:pad] = jnp.where(pos_z > 0, below,
                                                              jnp.zeros_like(below))
                    top = jnp.minimum(start + span, grown_ref.shape[2] - pad)
                    above = grown_ref[rows_x, rows_y, pl.ds(pl.multiple_of(top, 128), pad)]
                    win_ref[shift_y, :, :, pad + span:lanes] = jnp.where(
                        pos_z < tiles_z - 1, above, jnp.zeros_like(above))

        for pair in range(pairs):
            acc = None
            for tap in range(9):
                shift_x, shift_y = tap // 3, tap % 3
                slab = win_ref[shift_y, shift_x:shift_x + TILE, :,
                               2 * CIN * pair:2 * CIN * pair + 4 * CIN]
                part = jnp.dot(slab.reshape(rows, 4 * CIN), band_ref[tap],
                               preferred_element_type=jnp.float32)
                acc = part if acc is None else acc + part
            conv_ref[2 * pair] = acc[:, :CMID]
            conv_ref[2 * pair + 1] = acc[:, CMID:]

        count = float(rows * TILE * (CMID // GROUPS))
        indicator = ind_ref[...]
        total = jnp.zeros((1, CMID), jnp.float32)
        for depth in range(1, TILE + 1):
            total = total + jnp.sum(conv_ref[depth], axis=0, keepdims=True)
        mean = group_sum(total, indicator) / count
        total = jnp.zeros((1, CMID), jnp.float32)
        for depth in range(1, TILE + 1):
            diff = conv_ref[depth] - mean
            total = total + jnp.sum(diff * diff, axis=0, keepdims=True)
        var = group_sum(total, indicator) / count
        scale = lax.rsqrt(var + EPS) * gamma_ref[...]
        shift = beta_ref[...]
        for depth in range(1, TILE + 1):
            conv_ref[depth] = jnp.maximum((conv_ref[depth] - mean) * scale + shift, 0.0)

        results = [jnp.zeros((half * half, COUT), jnp.float32) for _ in range(half)]
        for pick_b in range(2):
            picked = conv_ref[:, pl.ds(pick_b, rows // 2, stride=2), :]
            for pick_a in range(2):
                corners = [
                    picked[depth].reshape(half, 2, half, CMID)[:, pick_a]
                    .reshape(half * half, CMID).astype(jnp.bfloat16)
                    for depth in range(1, TILE + 1)
                ]
                weight = down_ref[pick_a * 2 + pick_b]
                for depth in range(half):
                    lhs = jnp.concatenate([corners[2 * depth], corners[2 * depth + 1]], axis=1)
                    results[depth] = results[depth] + jnp.dot(
                        lhs, weight, preferred_element_type=jnp.float32)
        bias = bias_ref[...]
        merged = jnp.concatenate([r + bias for r in results], axis=1)
        out_ref[...] = merged.reshape(half, half, half * COUT).astype(jnp.bfloat16)

    @pl.when(flag == 0)
    def _():
        out_ref[...] = jnp.zeros(out_ref.shape, out_ref.dtype)


def shards(volume, tissue, w_conv, gamma, beta, w_down, b_down):
    own_index = lax.axis_index("gx")
    size_x, size_y, merged = volume.shape
    size_z = merged // CIN
    tiles_x, tiles_y, tiles_z = size_x // TILE, size_y // TILE, size_z // TILE
    tile_count = tiles_x * tiles_y * tiles_z
    half = TILE // 2
    grown = with_halo(volume, (("gx", 0), ("gy", 1)), 1)
    band = build_band(w_conv)
    lane = jnp.arange(CMID, dtype=jnp.int32)
    group_size = CMID // GROUPS
    indicator = (lane[:, None] // group_size == lane[None, :] // group_size).astype(jnp.bfloat16)
    down = w_down.reshape(4, 2 * CMID, COUT)
    own_tissue = lax.dynamic_slice_in_dim(tissue, own_index * tiles_x, tiles_x, 0)
    flags = own_tissue.reshape(tile_count).astype(jnp.int32)

    full = lambda shape: pl.BlockSpec(shape, lambda i, j, k, f: (0,) * len(shape))
    grid_spec = pltpu.PrefetchScalarGridSpec(
        num_scalar_prefetch=1,
        grid=(tiles_x, tiles_y, tiles_z),
        in_specs=[
            full(grown.shape),
            full((9, 4 * CIN, 2 * CMID)),
            full((CMID, CMID)),
            full((1, CMID)),
            full((1, CMID)),
            full((4, 2 * CMID, COUT)),
            full((1, COUT)),
        ],
        out_specs=pl.BlockSpec((half, half, half * COUT), lambda i, j, k, f: (i, j, k)),
        scratch_shapes=[
            pltpu.VMEM((3, TILE + 2, TILE, (TILE + 4) * CIN), jnp.bfloat16),
            pltpu.VMEM((TILE + 2, TILE * TILE, CMID), jnp.float32),
        ],
    )
    return pl.pallas_call(
        tile_kernel,
        grid_spec=grid_spec,
        out_shape=jax.ShapeDtypeStruct((size_x // 2, size_y // 2, size_z // 2 * COUT),
                                       jnp.bfloat16),
    )(
        flags,
        grown,
        band,
        indicator,
        gamma.reshape(1, CMID),
        beta.reshape(1, CMID),
        down,
        b_down.reshape(1, COUT),
    )


def solution(mesh):
    in_specs = (P("gx", "gy", None), P(None, "gy", None), P(), P(), P(), P(), P())
    out_specs = P("gx", "gy", None)
    return jax.shard_map(shards, mesh=mesh, in_specs=in_specs, out_specs=out_specs, check_vma=False)
```

```python
import jax
import jax.numpy as jnp
from jax import lax
from jax.experimental import pallas as pl
from jax.experimental.pallas import tpu as pltpu
from jax.sharding import PartitionSpec as P

CIN = 64
CMID = 128
COUT = 128
GROUPS = 8
TILE = 16
EPS = 1e-05


def neighbour(block, step_x, step_y):
    count_x, count_y = lax.axis_size("gx"), lax.axis_size("gy")
    pairs = []
    for ix in range(count_x):
        for iy in range(count_y):
            tx, ty = ix + step_x, iy + step_y
            if 0 <= tx < count_x and 0 <= ty < count_y:
                pairs.append((ix * count_y + iy, tx * count_y + ty))
    return lax.ppermute(block, ("gx", "gy"), pairs)


def shifted_halo(block):
    low_x = neighbour(block[-1:], 1, 0)
    high_x = neighbour(block[:1], -1, 0)
    low_y = neighbour(block[:, -1:], 0, 1)
    high_y = neighbour(block[:, :1], 0, -1)
    corner_ll = neighbour(block[-1:, -1:], 1, 1)
    corner_lh = neighbour(block[-1:, :1], 1, -1)
    corner_hl = neighbour(block[:1, -1:], -1, 1)
    corner_hh = neighbour(block[:1, :1], -1, -1)
    grown = jnp.concatenate([
        jnp.concatenate([corner_ll, low_x, corner_lh], axis=1),
        jnp.concatenate([low_y, block, high_y], axis=1),
        jnp.concatenate([corner_hl, high_x, corner_hh], axis=1),
    ], axis=0)
    size_y = block.shape[1]
    return jnp.stack([grown[:, dy:dy + size_y] for dy in range(3)])


def build_band(w_conv):
    in_pos = jnp.arange(4, dtype=jnp.int32)[:, None, None]
    out_pos = jnp.arange(2, dtype=jnp.int32)[None, :, None]
    taps = jnp.arange(3, dtype=jnp.int32)[None, None, :]
    select = (in_pos - out_pos == taps).astype(jnp.float32)
    band = jnp.einsum("zod,xydcm->xyzcom", select, w_conv.astype(jnp.float32))
    return band.reshape(9, 4 * CIN, 2 * CMID).astype(jnp.bfloat16)


def group_sum(row, indicator):
    row = jnp.broadcast_to(row, (8, row.shape[1]))
    total = jnp.zeros(row.shape, jnp.float32)
    rest = row
    for _ in range(3):
        piece = rest.astype(jnp.bfloat16)
        total = total + jnp.dot(piece, indicator, preferred_element_type=jnp.float32)
        rest = rest - piece.astype(jnp.float32)
    return total[0:1]


def tile_kernel(flags_ref, grown_ref, band_ref, ind_ref, gamma_ref, beta_ref, down_ref,
                bias_ref, out_ref, conv_ref):
    pos_x, pos_y, pos_z = pl.program_id(0), pl.program_id(1), pl.program_id(2)
    tiles_y, tiles_z = pl.num_programs(1), pl.num_programs(2)
    flag = flags_ref[(pos_x * tiles_y + pos_y) * tiles_z + pos_z]
    rows = TILE * TILE
    half = TILE // 2
    pairs = half + 1
    span = TILE * CIN
    pad = 2 * CIN
    start = pos_z * span

    def pair_conv(pair, offset, width, band_lo):
        lane_start = pl.multiple_of(start + offset, 128)
        acc = None
        for tap in range(9):
            shift_x, shift_y = tap // 3, tap % 3
            slab = grown_ref[shift_y, shift_x:shift_x + TILE, :, pl.ds(lane_start, width)]
            part = jnp.dot(slab.reshape(rows, width), band_ref[tap, band_lo:band_lo + width, :],
                           preferred_element_type=jnp.float32)
            acc = part if acc is None else acc + part
        conv_ref[2 * pair] = acc[:, :CMID]
        conv_ref[2 * pair + 1] = acc[:, CMID:]

    @pl.when(flag > 0)
    def _():
        @pl.when(pos_z > 0)
        def _():
            pair_conv(0, -pad, 2 * pad, 0)

        @pl.when(pos_z == 0)
        def _():
            pair_conv(0, 0, pad, pad)

        for pair in range(1, pairs - 1):
            pair_conv(pair, pad * (pair - 1), 2 * pad, 0)

        @pl.when(pos_z < tiles_z - 1)
        def _():
            pair_conv(pairs - 1, pad * (pairs - 2), 2 * pad, 0)

        @pl.when(pos_z == tiles_z - 1)
        def _():
            pair_conv(pairs - 1, pad * (pairs - 2), pad, 0)

        count = float(rows * TILE * (CMID // GROUPS))
        indicator = ind_ref[...]
        total = jnp.zeros((1, CMID), jnp.float32)
        for depth in range(1, TILE + 1):
            total = total + jnp.sum(conv_ref[depth], axis=0, keepdims=True)
        mean = group_sum(total, indicator) / count
        total = jnp.zeros((1, CMID), jnp.float32)
        for depth in range(1, TILE + 1):
            diff = conv_ref[depth] - mean
            total = total + jnp.sum(diff * diff, axis=0, keepdims=True)
        var = group_sum(total, indicator) / count
        scale = lax.rsqrt(var + EPS) * gamma_ref[...]
        shift = beta_ref[...]
        for depth in range(1, TILE + 1):
            conv_ref[depth] = jnp.maximum((conv_ref[depth] - mean) * scale + shift, 0.0)

        results = [jnp.zeros((half * half, COUT), jnp.float32) for _ in range(half)]
        for pick_b in range(2):
            picked = conv_ref[:, pl.ds(pick_b, rows // 2, stride=2), :]
            for pick_a in range(2):
                corners = [
                    picked[depth].reshape(half, 2, half, CMID)[:, pick_a]
                    .reshape(half * half, CMID).astype(jnp.bfloat16)
                    for depth in range(1, TILE + 1)
                ]
                weight = down_ref[pick_a * 2 + pick_b]
                for depth in range(half):
                    lhs = jnp.concatenate([corners[2 * depth], corners[2 * depth + 1]], axis=1)
                    results[depth] = results[depth] + jnp.dot(
                        lhs, weight, preferred_element_type=jnp.float32)
        bias = bias_ref[...]
        merged = jnp.concatenate([r + bias for r in results], axis=1)
        out_ref[...] = merged.reshape(half, half, half * COUT).astype(jnp.bfloat16)

    @pl.when(flag == 0)
    def _():
        out_ref[...] = jnp.zeros(out_ref.shape, out_ref.dtype)


def shards(volume, tissue, w_conv, gamma, beta, w_down, b_down):
    own_index = lax.axis_index("gx")
    size_x, size_y, merged = volume.shape
    size_z = merged // CIN
    tiles_x, tiles_y, tiles_z = size_x // TILE, size_y // TILE, size_z // TILE
    tile_count = tiles_x * tiles_y * tiles_z
    half = TILE // 2
    grown = shifted_halo(volume)
    band = build_band(w_conv)
    lane = jnp.arange(CMID, dtype=jnp.int32)
    group_size = CMID // GROUPS
    indicator = (lane[:, None] // group_size == lane[None, :] // group_size).astype(jnp.bfloat16)
    down = w_down.reshape(4, 2 * CMID, COUT)
    own_tissue = lax.dynamic_slice_in_dim(tissue, own_index * tiles_x, tiles_x, 0)
    flags = own_tissue.reshape(tile_count).astype(jnp.int32)

    full = lambda shape: pl.BlockSpec(shape, lambda i, j, k, f: (0,) * len(shape))
    grid_spec = pltpu.PrefetchScalarGridSpec(
        num_scalar_prefetch=1,
        grid=(tiles_x, tiles_y, tiles_z),
        in_specs=[
            pl.BlockSpec((pl.Element(3), pl.Element(TILE + 2), pl.Element(TILE),
                          pl.Element(merged)),
                         lambda i, j, k, f: (0, i * TILE, j * TILE, 0)),
            full((9, 4 * CIN, 2 * CMID)),
            full((CMID, CMID)),
            full((1, CMID)),
            full((1, CMID)),
            full((4, 2 * CMID, COUT)),
            full((1, COUT)),
        ],
        out_specs=pl.BlockSpec((half, half, half * COUT), lambda i, j, k, f: (i, j, k)),
        scratch_shapes=[pltpu.VMEM((TILE + 2, TILE * TILE, CMID), jnp.float32)],
    )
    return pl.pallas_call(
        tile_kernel,
        grid_spec=grid_spec,
        out_shape=jax.ShapeDtypeStruct((size_x // 2, size_y // 2, size_z // 2 * COUT),
                                       jnp.bfloat16),
    )(
        flags,
        grown,
        band,
        indicator,
        gamma.reshape(1, CMID),
        beta.reshape(1, CMID),
        down,
        b_down.reshape(1, COUT),
    )


def solution(mesh):
    in_specs = (P("gx", "gy", None), P(None, "gy", None), P(), P(), P(), P(), P())
    out_specs = P("gx", "gy", None)
    return jax.shard_map(shards, mesh=mesh, in_specs=in_specs, out_specs=out_specs, check_vma=False)
```

```python
import jax
import jax.numpy as jnp
from jax import lax
from jax.experimental import pallas as pl
from jax.experimental.pallas import tpu as pltpu
from jax.sharding import PartitionSpec as P

CIN = 64
CMID = 128
COUT = 128
GROUPS = 8
TILE = 16
EPS = 1e-05


def neighbour(block, step_x, step_y):
    count_x, count_y = lax.axis_size("gx"), lax.axis_size("gy")
    pairs = []
    for ix in range(count_x):
        for iy in range(count_y):
            tx, ty = ix + step_x, iy + step_y
            if 0 <= tx < count_x and 0 <= ty < count_y:
                pairs.append((ix * count_y + iy, tx * count_y + ty))
    return lax.ppermute(block, ("gx", "gy"), pairs)


def grown_block(block):
    low_x = neighbour(block[-1], 1, 0)
    high_x = neighbour(block[0], -1, 0)
    column_hi = jnp.concatenate([low_x[None, -1], block[:, -1], high_x[None, -1]], axis=0)
    column_lo = jnp.concatenate([low_x[None, 0], block[:, 0], high_x[None, 0]], axis=0)
    low_y = neighbour(column_hi, 0, 1)
    high_y = neighbour(column_lo, 0, -1)
    middle = jnp.concatenate([low_x[None], block, high_x[None]], axis=0)
    return jnp.concatenate([low_y[:, None], middle, high_y[:, None]], axis=1)


def build_band(w_conv):
    in_pos = jnp.arange(4, dtype=jnp.int32)[:, None, None]
    out_pos = jnp.arange(2, dtype=jnp.int32)[None, :, None]
    taps = jnp.arange(3, dtype=jnp.int32)[None, None, :]
    select = (in_pos - out_pos == taps).astype(jnp.float32)
    band = jnp.einsum("zod,xydcm->xyzcom", select, w_conv.astype(jnp.float32))
    return band.reshape(9, 4 * CIN, 2 * CMID).astype(jnp.bfloat16)


def group_sum(row, indicator):
    row = jnp.broadcast_to(row, (8, row.shape[1]))
    total = jnp.zeros(row.shape, jnp.float32)
    rest = row
    for _ in range(3):
        piece = rest.astype(jnp.bfloat16)
        total = total + jnp.dot(piece, indicator, preferred_element_type=jnp.float32)
        rest = rest - piece.astype(jnp.float32)
    return total[0:1]


def tile_kernel(flags_ref, grown_ref, band_ref, ind_ref, gamma_ref, beta_ref, down_ref,
                bias_ref, out_ref, conv_ref):
    pos_x, pos_y, pos_z = pl.program_id(0), pl.program_id(1), pl.program_id(2)
    tiles_y, tiles_z = pl.num_programs(1), pl.num_programs(2)
    flag = flags_ref[(pos_x * tiles_y + pos_y) * tiles_z + pos_z]
    rows = TILE * TILE
    half = TILE // 2
    pairs = half + 1
    span = TILE * CIN
    pad = 2 * CIN
    start = pos_z * span

    def pair_conv(col, pair, offset, width, band_lo):
        lane_start = pl.multiple_of(start + offset, 128)
        acc = None
        for tap in range(9):
            shift_x, shift_y = tap // 3, tap % 3
            slab = grown_ref[shift_x:shift_x + TILE, pl.ds(col * TILE + shift_y, TILE),
                             pl.ds(lane_start, width)]
            part = jnp.dot(slab.reshape(rows, width), band_ref[tap, band_lo:band_lo + width, :],
                           preferred_element_type=jnp.float32)
            acc = part if acc is None else acc + part
        conv_ref[2 * pair] = acc[:, :CMID]
        conv_ref[2 * pair + 1] = acc[:, CMID:]

    def tile_conv(col):
        @pl.when(pos_z > 0)
        def _():
            pair_conv(col, 0, -pad, 2 * pad, 0)

        @pl.when(pos_z == 0)
        def _():
            pair_conv(col, 0, 0, pad, pad)

        for pair in range(1, pairs - 1):
            pair_conv(col, pair, pad * (pair - 1), 2 * pad, 0)

        @pl.when(pos_z < tiles_z - 1)
        def _():
            pair_conv(col, pairs - 1, pad * (pairs - 2), 2 * pad, 0)

        @pl.when(pos_z == tiles_z - 1)
        def _():
            pair_conv(col, pairs - 1, pad * (pairs - 2), pad, 0)

    @pl.when(flag > 0)
    def _():
        for col in range(grown_ref.shape[1] // TILE):
            @pl.when(pos_y == col)
            def _():
                tile_conv(col)

        count = float(rows * TILE * (CMID // GROUPS))
        indicator = ind_ref[...]
        total = jnp.zeros((1, CMID), jnp.float32)
        for depth in range(1, TILE + 1):
            total = total + jnp.sum(conv_ref[depth], axis=0, keepdims=True)
        mean = group_sum(total, indicator) / count
        total = jnp.zeros((1, CMID), jnp.float32)
        for depth in range(1, TILE + 1):
            diff = conv_ref[depth] - mean
            total = total + jnp.sum(diff * diff, axis=0, keepdims=True)
        var = group_sum(total, indicator) / count
        scale = lax.rsqrt(var + EPS) * gamma_ref[...]
        shift = beta_ref[...]
        for depth in range(1, TILE + 1):
            conv_ref[depth] = jnp.maximum((conv_ref[depth] - mean) * scale + shift, 0.0)

        results = [jnp.zeros((half * half, COUT), jnp.float32) for _ in range(half)]
        for pick_b in range(2):
            picked = conv_ref[:, pl.ds(pick_b, rows // 2, stride=2), :]
            for pick_a in range(2):
                corners = [
                    picked[depth].reshape(half, 2, half, CMID)[:, pick_a]
                    .reshape(half * half, CMID).astype(jnp.bfloat16)
                    for depth in range(1, TILE + 1)
                ]
                weight = down_ref[pick_a * 2 + pick_b]
                for depth in range(half):
                    lhs = jnp.concatenate([corners[2 * depth], corners[2 * depth + 1]], axis=1)
                    results[depth] = results[depth] + jnp.dot(
                        lhs, weight, preferred_element_type=jnp.float32)
        bias = bias_ref[...]
        merged = jnp.concatenate([r + bias for r in results], axis=1)
        out_ref[...] = merged.reshape(half, half, half * COUT).astype(jnp.bfloat16)

    @pl.when(flag == 0)
    def _():
        out_ref[...] = jnp.zeros(out_ref.shape, out_ref.dtype)


def shards(volume, tissue, w_conv, gamma, beta, w_down, b_down):
    own_index = lax.axis_index("gx")
    size_x, size_y, merged = volume.shape
    size_z = merged // CIN
    tiles_x, tiles_y, tiles_z = size_x // TILE, size_y // TILE, size_z // TILE
    tile_count = tiles_x * tiles_y * tiles_z
    half = TILE // 2
    grown = grown_block(volume)
    band = build_band(w_conv)
    lane = jnp.arange(CMID, dtype=jnp.int32)
    group_size = CMID // GROUPS
    indicator = (lane[:, None] // group_size == lane[None, :] // group_size).astype(jnp.bfloat16)
    down = w_down.reshape(4, 2 * CMID, COUT)
    own_tissue = lax.dynamic_slice_in_dim(tissue, own_index * tiles_x, tiles_x, 0)
    flags = own_tissue.reshape(tile_count).astype(jnp.int32)

    full = lambda shape: pl.BlockSpec(shape, lambda i, j, k, f: (0,) * len(shape))
    grid_spec = pltpu.PrefetchScalarGridSpec(
        num_scalar_prefetch=1,
        grid=(tiles_x, tiles_y, tiles_z),
        in_specs=[
            pl.BlockSpec((pl.Element(TILE + 2), pl.Element(size_y + 2), pl.Element(merged)),
                         lambda i, j, k, f: (i * TILE, 0, 0)),
            full((9, 4 * CIN, 2 * CMID)),
            full((CMID, CMID)),
            full((1, CMID)),
            full((1, CMID)),
            full((4, 2 * CMID, COUT)),
            full((1, COUT)),
        ],
        out_specs=pl.BlockSpec((half, half, half * COUT), lambda i, j, k, f: (i, j, k)),
        scratch_shapes=[pltpu.VMEM((TILE + 2, TILE * TILE, CMID), jnp.float32)],
    )
    return pl.pallas_call(
        tile_kernel,
        grid_spec=grid_spec,
        out_shape=jax.ShapeDtypeStruct((size_x // 2, size_y // 2, size_z // 2 * COUT),
                                       jnp.bfloat16),
    )(
        flags,
        grown,
        band,
        indicator,
        gamma.reshape(1, CMID),
        beta.reshape(1, CMID),
        down,
        b_down.reshape(1, COUT),
    )


def solution(mesh):
    in_specs = (P("gx", "gy", None), P(None, "gy", None), P(), P(), P(), P(), P())
    out_specs = P("gx", "gy", None)
    return jax.shard_map(shards, mesh=mesh, in_specs=in_specs, out_specs=out_specs, check_vma=False)
```

```python
import jax
import jax.numpy as jnp
from jax import lax
from jax.experimental import pallas as pl
from jax.experimental.pallas import tpu as pltpu
from jax.sharding import PartitionSpec as P

CIN = 64
CMID = 128
COUT = 128
GROUPS = 8
TILE = 16
EPS = 1e-05


def neighbour(block, step_x, step_y):
    count_x, count_y = lax.axis_size("gx"), lax.axis_size("gy")
    pairs = []
    for ix in range(count_x):
        for iy in range(count_y):
            tx, ty = ix + step_x, iy + step_y
            if 0 <= tx < count_x and 0 <= ty < count_y:
                pairs.append((ix * count_y + iy, tx * count_y + ty))
    return lax.ppermute(block, ("gx", "gy"), pairs)


def grown_block(block):
    low_x = neighbour(block[-1], 1, 0)
    high_x = neighbour(block[0], -1, 0)
    column_hi = jnp.concatenate([low_x[None, -1], block[:, -1], high_x[None, -1]], axis=0)
    column_lo = jnp.concatenate([low_x[None, 0], block[:, 0], high_x[None, 0]], axis=0)
    low_y = neighbour(column_hi, 0, 1)
    high_y = neighbour(column_lo, 0, -1)
    middle = jnp.concatenate([low_x[None], block, high_x[None]], axis=0)
    return jnp.concatenate([low_y[:, None], middle, high_y[:, None]], axis=1)


def build_band(w_conv):
    taps = w_conv.reshape(9, 3, CIN, CMID)
    zero = jnp.zeros((9, CIN, CMID), w_conv.dtype)
    first = jnp.concatenate([taps[:, 0], taps[:, 1], taps[:, 2], zero], axis=1)
    second = jnp.concatenate([zero, taps[:, 0], taps[:, 1], taps[:, 2]], axis=1)
    return jnp.concatenate([first, second], axis=2)


def group_sum(row, indicator):
    row = jnp.broadcast_to(row, (8, row.shape[1]))
    total = jnp.zeros(row.shape, jnp.float32)
    rest = row
    for _ in range(3):
        piece = rest.astype(jnp.bfloat16)
        total = total + jnp.dot(piece, indicator, preferred_element_type=jnp.float32)
        rest = rest - piece.astype(jnp.float32)
    return total[0:1]


def tile_kernel(flags_ref, grown_ref, band_ref, ind_ref, gamma_ref, beta_ref, down_ref,
                bias_ref, out_ref, conv_ref):
    pos_x, pos_y, pos_z = pl.program_id(0), pl.program_id(1), pl.program_id(2)
    tiles_y, tiles_z = pl.num_programs(1), pl.num_programs(2)
    flag = flags_ref[(pos_x * tiles_y + pos_y) * tiles_z + pos_z]
    rows = TILE * TILE
    half = TILE // 2
    pairs = half + 1
    span = TILE * CIN
    pad = 2 * CIN
    start = pos_z * span

    def pair_conv(col, pair, offset, width, band_lo):
        lane_start = pl.multiple_of(start + offset, 128)
        acc = None
        for tap in range(9):
            shift_x, shift_y = tap // 3, tap % 3
            slab = grown_ref[shift_x:shift_x + TILE, pl.ds(col * TILE + shift_y, TILE),
                             pl.ds(lane_start, width)]
            part = jnp.dot(slab.reshape(rows, width), band_ref[tap, band_lo:band_lo + width, :],
                           preferred_element_type=jnp.float32)
            acc = part if acc is None else acc + part
        conv_ref[2 * pair] = acc[:, :CMID]
        conv_ref[2 * pair + 1] = acc[:, CMID:]

    def tile_conv(col):
        @pl.when(pos_z > 0)
        def _():
            pair_conv(col, 0, -pad, 2 * pad, 0)

        @pl.when(pos_z == 0)
        def _():
            pair_conv(col, 0, 0, pad, pad)

        for pair in range(1, pairs - 1):
            pair_conv(col, pair, pad * (pair - 1), 2 * pad, 0)

        @pl.when(pos_z < tiles_z - 1)
        def _():
            pair_conv(col, pairs - 1, pad * (pairs - 2), 2 * pad, 0)

        @pl.when(pos_z == tiles_z - 1)
        def _():
            pair_conv(col, pairs - 1, pad * (pairs - 2), pad, 0)

    @pl.when(flag > 0)
    def _():
        for col in range(grown_ref.shape[1] // TILE):
            @pl.when(pos_y == col)
            def _():
                tile_conv(col)

        count = float(rows * TILE * (CMID // GROUPS))
        indicator = ind_ref[...]
        total = jnp.zeros((1, CMID), jnp.float32)
        for depth in range(1, TILE + 1):
            total = total + jnp.sum(conv_ref[depth], axis=0, keepdims=True)
        mean = group_sum(total, indicator) / count
        total = jnp.zeros((1, CMID), jnp.float32)
        for depth in range(1, TILE + 1):
            diff = conv_ref[depth] - mean
            total = total + jnp.sum(diff * diff, axis=0, keepdims=True)
        var = group_sum(total, indicator) / count
        scale = lax.rsqrt(var + EPS) * gamma_ref[...]
        shift = beta_ref[...]

        results = [None] * half
        for pick_b in range(2):
            picked = conv_ref[:, pl.ds(pick_b, rows // 2, stride=2), :]
            normed = [
                jnp.maximum((picked[depth] - mean) * scale + shift, 0.0)
                .reshape(half, 2, half, CMID)
                for depth in range(1, TILE + 1)
            ]
            for pick_a in range(2):
                corners = [n[:, pick_a].reshape(half * half, CMID).astype(jnp.bfloat16)
                           for n in normed]
                lhs = jnp.concatenate([
                    jnp.concatenate([corners[2 * depth], corners[2 * depth + 1]], axis=1)
                    for depth in range(half)
                ], axis=0)
                part = jnp.dot(lhs, down_ref[pick_a * 2 + pick_b],
                               preferred_element_type=jnp.float32)
                for depth in range(half):
                    piece = part[half * half * depth:half * half * (depth + 1)]
                    results[depth] = piece if results[depth] is None else results[depth] + piece
        bias = bias_ref[...]
        merged = jnp.concatenate([r + bias for r in results], axis=1)
        out_ref[...] = merged.reshape(half, half, half * COUT).astype(jnp.bfloat16)

    @pl.when(flag == 0)
    def _():
        out_ref[...] = jnp.zeros(out_ref.shape, out_ref.dtype)


def shards(volume, tissue, w_conv, gamma, beta, w_down, b_down):
    own_index = lax.axis_index("gx")
    size_x, size_y, merged = volume.shape
    size_z = merged // CIN
    tiles_x, tiles_y, tiles_z = size_x // TILE, size_y // TILE, size_z // TILE
    tile_count = tiles_x * tiles_y * tiles_z
    half = TILE // 2
    grown = grown_block(volume)
    band = build_band(w_conv)
    lane = jnp.arange(CMID, dtype=jnp.int32)
    group_size = CMID // GROUPS
    indicator = (lane[:, None] // group_size == lane[None, :] // group_size).astype(jnp.bfloat16)
    down = w_down.reshape(4, 2 * CMID, COUT)
    own_tissue = lax.dynamic_slice_in_dim(tissue, own_index * tiles_x, tiles_x, 0)
    flags = own_tissue.reshape(tile_count).astype(jnp.int32)

    full = lambda shape: pl.BlockSpec(shape, lambda i, j, k, f: (0,) * len(shape))
    grid_spec = pltpu.PrefetchScalarGridSpec(
        num_scalar_prefetch=1,
        grid=(tiles_x, tiles_y, tiles_z),
        in_specs=[
            pl.BlockSpec((pl.Element(TILE + 2), pl.Element(size_y + 2), pl.Element(merged)),
                         lambda i, j, k, f: (i * TILE, 0, 0)),
            full((9, 4 * CIN, 2 * CMID)),
            full((CMID, CMID)),
            full((1, CMID)),
            full((1, CMID)),
            full((4, 2 * CMID, COUT)),
            full((1, COUT)),
        ],
        out_specs=pl.BlockSpec((half, half, half * COUT), lambda i, j, k, f: (i, j, k)),
        scratch_shapes=[pltpu.VMEM((TILE + 2, TILE * TILE, CMID), jnp.float32)],
    )
    return pl.pallas_call(
        tile_kernel,
        grid_spec=grid_spec,
        out_shape=jax.ShapeDtypeStruct((size_x // 2, size_y // 2, size_z // 2 * COUT),
                                       jnp.bfloat16),
    )(
        flags,
        grown,
        band,
        indicator,
        gamma.reshape(1, CMID),
        beta.reshape(1, CMID),
        down,
        b_down.reshape(1, COUT),
    )


def solution(mesh):
    in_specs = (P("gx", "gy", None), P(None, "gy", None), P(), P(), P(), P(), P())
    out_specs = P("gx", "gy", None)
    return jax.shard_map(shards, mesh=mesh, in_specs=in_specs, out_specs=out_specs, check_vma=False)
```

```python
import jax
import jax.numpy as jnp
from jax import lax
from jax.experimental import pallas as pl
from jax.experimental.pallas import tpu as pltpu
from jax.sharding import PartitionSpec as P

CIN = 64
CMID = 128
COUT = 128
GROUPS = 8
TILE = 16
EPS = 1e-05


def neighbour(block, step_x, step_y):
    count_x, count_y = lax.axis_size("gx"), lax.axis_size("gy")
    pairs = []
    for ix in range(count_x):
        for iy in range(count_y):
            tx, ty = ix + step_x, iy + step_y
            if 0 <= tx < count_x and 0 <= ty < count_y:
                pairs.append((ix * count_y + iy, tx * count_y + ty))
    return lax.ppermute(block, ("gx", "gy"), pairs)


def grown_block(block):
    low_x = neighbour(block[-1], 1, 0)
    high_x = neighbour(block[0], -1, 0)
    column_hi = jnp.concatenate([low_x[None, -1], block[:, -1], high_x[None, -1]], axis=0)
    column_lo = jnp.concatenate([low_x[None, 0], block[:, 0], high_x[None, 0]], axis=0)
    low_y = neighbour(column_hi, 0, 1)
    high_y = neighbour(column_lo, 0, -1)
    middle = jnp.concatenate([low_x[None], block, high_x[None]], axis=0)
    return jnp.concatenate([low_y[:, None], middle, high_y[:, None]], axis=1)


def build_band(w_conv):
    taps = w_conv.reshape(9, 3, CIN, CMID)
    zero = jnp.zeros((9, CIN, CMID), w_conv.dtype)
    first = jnp.concatenate([taps[:, 0], taps[:, 1], taps[:, 2], zero], axis=1)
    second = jnp.concatenate([zero, taps[:, 0], taps[:, 1], taps[:, 2]], axis=1)
    return jnp.concatenate([first, second], axis=2)


def group_sum(row, indicator):
    row = jnp.broadcast_to(row, (8, row.shape[1]))
    total = jnp.zeros(row.shape, jnp.float32)
    rest = row
    for _ in range(3):
        piece = rest.astype(jnp.bfloat16)
        total = total + jnp.dot(piece, indicator, preferred_element_type=jnp.float32)
        rest = rest - piece.astype(jnp.float32)
    return total[0:1]


def tile_kernel(flags_ref, grown_ref, band_ref, wide_ref, ind_ref, gamma_ref, beta_ref, down_ref,
                bias_ref, out_ref, conv_ref):
    pos_x, pos_y, pos_z = pl.program_id(0), pl.program_id(1), pl.program_id(2)
    tiles_y, tiles_z = pl.num_programs(1), pl.num_programs(2)
    flag = flags_ref[(pos_x * tiles_y + pos_y) * tiles_z + pos_z]
    rows = TILE * TILE
    half = TILE // 2
    pairs = half + 1
    span = TILE * CIN
    pad = 2 * CIN
    start = pos_z * span

    def pair_conv(col, pair, offset, width, band_lo):
        lane_start = pl.multiple_of(start + offset, 128)
        acc = None
        for tap in range(9):
            shift_x, shift_y = tap // 3, tap % 3
            slab = grown_ref[shift_x:shift_x + TILE, pl.ds(col * TILE + shift_y, TILE),
                             pl.ds(lane_start, width)]
            part = jnp.dot(slab.reshape(rows, width), band_ref[tap, band_lo:band_lo + width, :],
                           preferred_element_type=jnp.float32)
            acc = part if acc is None else acc + part
        conv_ref[2 * pair] = acc[:, :CMID]
        conv_ref[2 * pair + 1] = acc[:, CMID:]

    def tile_conv(col):
        @pl.when(pos_z > 0)
        def _():
            pair_conv(col, 0, -pad, 2 * pad, 0)

        @pl.when(pos_z == 0)
        def _():
            pair_conv(col, 0, 0, pad, pad)

        for pair in range(1, pairs - 1):
            lane_start = pl.multiple_of(start + pad * (pair - 1), 128)
            slabs = [
                grown_ref[tap // 3:tap // 3 + TILE, pl.ds(col * TILE + tap % 3, TILE),
                          pl.ds(lane_start, 2 * pad)].reshape(rows, 2 * pad)
                for tap in range(9)
            ]
            acc = jnp.dot(jnp.concatenate(slabs, axis=1), wide_ref[...],
                          preferred_element_type=jnp.float32)
            conv_ref[2 * pair] = acc[:, :CMID]
            conv_ref[2 * pair + 1] = acc[:, CMID:]

        @pl.when(pos_z < tiles_z - 1)
        def _():
            pair_conv(col, pairs - 1, pad * (pairs - 2), 2 * pad, 0)

        @pl.when(pos_z == tiles_z - 1)
        def _():
            pair_conv(col, pairs - 1, pad * (pairs - 2), pad, 0)

    @pl.when(flag > 0)
    def _():
        for col in range(grown_ref.shape[1] // TILE):
            @pl.when(pos_y == col)
            def _():
                tile_conv(col)

        count = float(rows * TILE * (CMID // GROUPS))
        indicator = ind_ref[...]
        total = jnp.zeros((1, CMID), jnp.float32)
        for depth in range(1, TILE + 1):
            total = total + jnp.sum(conv_ref[depth], axis=0, keepdims=True)
        mean = group_sum(total, indicator) / count
        total = jnp.zeros((1, CMID), jnp.float32)
        for depth in range(1, TILE + 1):
            diff = conv_ref[depth] - mean
            total = total + jnp.sum(diff * diff, axis=0, keepdims=True)
        var = group_sum(total, indicator) / count
        scale = lax.rsqrt(var + EPS) * gamma_ref[...]
        shift = beta_ref[...]

        results = [None] * half
        for pick_b in range(2):
            picked = conv_ref[:, pl.ds(pick_b, rows // 2, stride=2), :]
            normed = [
                jnp.maximum((picked[depth] - mean) * scale + shift, 0.0)
                .reshape(half, 2, half, CMID)
                for depth in range(1, TILE + 1)
            ]
            for pick_a in range(2):
                corners = [n[:, pick_a].reshape(half * half, CMID).astype(jnp.bfloat16)
                           for n in normed]
                lhs = jnp.concatenate([
                    jnp.concatenate([corners[2 * depth], corners[2 * depth + 1]], axis=1)
                    for depth in range(half)
                ], axis=0)
                part = jnp.dot(lhs, down_ref[pick_a * 2 + pick_b],
                               preferred_element_type=jnp.float32)
                for depth in range(half):
                    piece = part[half * half * depth:half * half * (depth + 1)]
                    results[depth] = piece if results[depth] is None else results[depth] + piece
        bias = bias_ref[...]
        merged = jnp.concatenate([r + bias for r in results], axis=1)
        out_ref[...] = merged.reshape(half, half, half * COUT).astype(jnp.bfloat16)

    @pl.when(flag == 0)
    def _():
        out_ref[...] = jnp.zeros(out_ref.shape, out_ref.dtype)


def shards(volume, tissue, w_conv, gamma, beta, w_down, b_down):
    own_index = lax.axis_index("gx")
    size_x, size_y, merged = volume.shape
    size_z = merged // CIN
    tiles_x, tiles_y, tiles_z = size_x // TILE, size_y // TILE, size_z // TILE
    tile_count = tiles_x * tiles_y * tiles_z
    half = TILE // 2
    grown = grown_block(volume)
    band = build_band(w_conv)
    lane = jnp.arange(CMID, dtype=jnp.int32)
    group_size = CMID // GROUPS
    indicator = (lane[:, None] // group_size == lane[None, :] // group_size).astype(jnp.bfloat16)
    down = w_down.reshape(4, 2 * CMID, COUT)
    own_tissue = lax.dynamic_slice_in_dim(tissue, own_index * tiles_x, tiles_x, 0)
    flags = own_tissue.reshape(tile_count).astype(jnp.int32)

    full = lambda shape: pl.BlockSpec(shape, lambda i, j, k, f: (0,) * len(shape))
    grid_spec = pltpu.PrefetchScalarGridSpec(
        num_scalar_prefetch=1,
        grid=(tiles_x, tiles_y, tiles_z),
        in_specs=[
            pl.BlockSpec((pl.Element(TILE + 2), pl.Element(size_y + 2), pl.Element(merged)),
                         lambda i, j, k, f: (i * TILE, 0, 0)),
            full((9, 4 * CIN, 2 * CMID)),
            full((9 * 4 * CIN, 2 * CMID)),
            full((CMID, CMID)),
            full((1, CMID)),
            full((1, CMID)),
            full((4, 2 * CMID, COUT)),
            full((1, COUT)),
        ],
        out_specs=pl.BlockSpec((half, half, half * COUT), lambda i, j, k, f: (i, j, k)),
        scratch_shapes=[pltpu.VMEM((TILE + 2, TILE * TILE, CMID), jnp.float32)],
    )
    return pl.pallas_call(
        tile_kernel,
        grid_spec=grid_spec,
        out_shape=jax.ShapeDtypeStruct((size_x // 2, size_y // 2, size_z // 2 * COUT),
                                       jnp.bfloat16),
    )(
        flags,
        grown,
        band,
        band.reshape(9 * 4 * CIN, 2 * CMID),
        indicator,
        gamma.reshape(1, CMID),
        beta.reshape(1, CMID),
        down,
        b_down.reshape(1, COUT),
    )


def solution(mesh):
    in_specs = (P("gx", "gy", None), P(None, "gy", None), P(), P(), P(), P(), P())
    out_specs = P("gx", "gy", None)
    return jax.shard_map(shards, mesh=mesh, in_specs=in_specs, out_specs=out_specs, check_vma=False)
```

```python
import jax
import jax.numpy as jnp
from jax import lax
from jax.experimental import pallas as pl
from jax.experimental.pallas import tpu as pltpu
from jax.sharding import PartitionSpec as P

CIN = 64
CMID = 128
COUT = 128
GROUPS = 8
TILE = 16
EPS = 1e-05


def neighbour(block, step_x, step_y):
    count_x, count_y = lax.axis_size("gx"), lax.axis_size("gy")
    pairs = []
    for ix in range(count_x):
        for iy in range(count_y):
            tx, ty = ix + step_x, iy + step_y
            if 0 <= tx < count_x and 0 <= ty < count_y:
                pairs.append((ix * count_y + iy, tx * count_y + ty))
    return lax.ppermute(block, ("gx", "gy"), pairs)


def grown_block(block):
    low_x = neighbour(block[-1], 1, 0)
    high_x = neighbour(block[0], -1, 0)
    column_hi = jnp.concatenate([low_x[None, -1], block[:, -1], high_x[None, -1]], axis=0)
    column_lo = jnp.concatenate([low_x[None, 0], block[:, 0], high_x[None, 0]], axis=0)
    low_y = neighbour(column_hi, 0, 1)
    high_y = neighbour(column_lo, 0, -1)
    middle = jnp.concatenate([low_x[None], block, high_x[None]], axis=0)
    return jnp.concatenate([low_y[:, None], middle, high_y[:, None]], axis=1)


def build_band(w_conv):
    taps = w_conv.reshape(9, 3, CIN, CMID)
    zero = jnp.zeros((9, CIN, CMID), w_conv.dtype)
    first = jnp.concatenate([taps[:, 0], taps[:, 1], taps[:, 2], zero], axis=1)
    second = jnp.concatenate([zero, taps[:, 0], taps[:, 1], taps[:, 2]], axis=1)
    return jnp.concatenate([first, second], axis=2)


def group_sum(row, indicator):
    row = jnp.broadcast_to(row, (8, row.shape[1]))
    total = jnp.zeros(row.shape, jnp.float32)
    rest = row
    for _ in range(3):
        piece = rest.astype(jnp.bfloat16)
        total = total + jnp.dot(piece, indicator, preferred_element_type=jnp.float32)
        rest = rest - piece.astype(jnp.float32)
    return total[0:1]


def tile_kernel(flags_ref, grown_ref, band_ref, ind_ref, gamma_ref, beta_ref, down_ref,
                bias_ref, out_ref, conv_ref):
    pos_x, pos_y, pos_z = pl.program_id(0), pl.program_id(1), pl.program_id(2)
    tiles_y, tiles_z = pl.num_programs(1), pl.num_programs(2)
    flag = flags_ref[(pos_x * tiles_y + pos_y) * tiles_z + pos_z]
    rows = TILE * TILE
    half = TILE // 2
    pairs = half + 1
    span = TILE * CIN
    pad = 2 * CIN
    start = pos_z * span

    def pair_conv(col, pair, offset, width, band_lo):
        lane_start = pl.multiple_of(start + offset, 128)
        acc = None
        for tap in range(9):
            shift_x, shift_y = tap // 3, tap % 3
            slab = grown_ref[shift_x:shift_x + TILE, pl.ds(col * TILE + shift_y, TILE),
                             pl.ds(lane_start, width)]
            part = jnp.dot(slab.reshape(rows, width), band_ref[tap, band_lo:band_lo + width, :],
                           preferred_element_type=jnp.float32)
            acc = part if acc is None else acc + part
        conv_ref[2 * pair] = acc[:, :CMID]
        conv_ref[2 * pair + 1] = acc[:, CMID:]

    def tile_conv(col):
        @pl.when(pos_z > 0)
        def _():
            pair_conv(col, 0, -pad, 2 * pad, 0)

        @pl.when(pos_z == 0)
        def _():
            pair_conv(col, 0, 0, pad, pad)

        for first in range(1, pairs - 1, 2):
            group = list(range(first, min(first + 2, pairs - 1)))
            acc = None
            for tap in range(9):
                shift_x, shift_y = tap // 3, tap % 3
                slabs = [
                    grown_ref[shift_x:shift_x + TILE, pl.ds(col * TILE + shift_y, TILE),
                              pl.ds(pl.multiple_of(start + pad * (pair - 1), 128), 2 * pad)]
                    .reshape(rows, 2 * pad)
                    for pair in group
                ]
                lhs = slabs[0] if len(slabs) == 1 else jnp.concatenate(slabs, axis=0)
                part = jnp.dot(lhs, band_ref[tap], preferred_element_type=jnp.float32)
                acc = part if acc is None else acc + part
            for index, pair in enumerate(group):
                conv_ref[2 * pair] = acc[rows * index:rows * (index + 1), :CMID]
                conv_ref[2 * pair + 1] = acc[rows * index:rows * (index + 1), CMID:]

        @pl.when(pos_z < tiles_z - 1)
        def _():
            pair_conv(col, pairs - 1, pad * (pairs - 2), 2 * pad, 0)

        @pl.when(pos_z == tiles_z - 1)
        def _():
            pair_conv(col, pairs - 1, pad * (pairs - 2), pad, 0)

    @pl.when(flag > 0)
    def _():
        for col in range(grown_ref.shape[1] // TILE):
            @pl.when(pos_y == col)
            def _():
                tile_conv(col)

        count = float(rows * TILE * (CMID // GROUPS))
        indicator = ind_ref[...]
        total = jnp.zeros((1, CMID), jnp.float32)
        for depth in range(1, TILE + 1):
            total = total + jnp.sum(conv_ref[depth], axis=0, keepdims=True)
        mean = group_sum(total, indicator) / count
        total = jnp.zeros((1, CMID), jnp.float32)
        for depth in range(1, TILE + 1):
            diff = conv_ref[depth] - mean
            total = total + jnp.sum(diff * diff, axis=0, keepdims=True)
        var = group_sum(total, indicator) / count
        scale = lax.rsqrt(var + EPS) * gamma_ref[...]
        shift = beta_ref[...]

        results = [None] * half
        for pick_b in range(2):
            picked = conv_ref[:, pl.ds(pick_b, rows // 2, stride=2), :]
            normed = [
                jnp.maximum((picked[depth] - mean) * scale + shift, 0.0)
                .reshape(half, 2, half, CMID)
                for depth in range(1, TILE + 1)
            ]
            for pick_a in range(2):
                corners = [n[:, pick_a].reshape(half * half, CMID).astype(jnp.bfloat16)
                           for n in normed]
                lhs = jnp.concatenate([
                    jnp.concatenate([corners[2 * depth], corners[2 * depth + 1]], axis=1)
                    for depth in range(half)
                ], axis=0)
                part = jnp.dot(lhs, down_ref[pick_a * 2 + pick_b],
                               preferred_element_type=jnp.float32)
                for depth in range(half):
                    piece = part[half * half * depth:half * half * (depth + 1)]
                    results[depth] = piece if results[depth] is None else results[depth] + piece
        bias = bias_ref[...]
        merged = jnp.concatenate([r + bias for r in results], axis=1)
        out_ref[...] = merged.reshape(half, half, half * COUT).astype(jnp.bfloat16)

    @pl.when(flag == 0)
    def _():
        out_ref[...] = jnp.zeros(out_ref.shape, out_ref.dtype)


def shards(volume, tissue, w_conv, gamma, beta, w_down, b_down):
    own_index = lax.axis_index("gx")
    size_x, size_y, merged = volume.shape
    size_z = merged // CIN
    tiles_x, tiles_y, tiles_z = size_x // TILE, size_y // TILE, size_z // TILE
    tile_count = tiles_x * tiles_y * tiles_z
    half = TILE // 2
    grown = grown_block(volume)
    band = build_band(w_conv)
    lane = jnp.arange(CMID, dtype=jnp.int32)
    group_size = CMID // GROUPS
    indicator = (lane[:, None] // group_size == lane[None, :] // group_size).astype(jnp.bfloat16)
    down = w_down.reshape(4, 2 * CMID, COUT)
    own_tissue = lax.dynamic_slice_in_dim(tissue, own_index * tiles_x, tiles_x, 0)
    flags = own_tissue.reshape(tile_count).astype(jnp.int32)

    full = lambda shape: pl.BlockSpec(shape, lambda i, j, k, f: (0,) * len(shape))
    grid_spec = pltpu.PrefetchScalarGridSpec(
        num_scalar_prefetch=1,
        grid=(tiles_x, tiles_y, tiles_z),
        in_specs=[
            pl.BlockSpec((pl.Element(TILE + 2), pl.Element(size_y + 2), pl.Element(merged)),
                         lambda i, j, k, f: (i * TILE, 0, 0)),
            full((9, 4 * CIN, 2 * CMID)),
            full((CMID, CMID)),
            full((1, CMID)),
            full((1, CMID)),
            full((4, 2 * CMID, COUT)),
            full((1, COUT)),
        ],
        out_specs=pl.BlockSpec((half, half, half * COUT), lambda i, j, k, f: (i, j, k)),
        scratch_shapes=[pltpu.VMEM((TILE + 2, TILE * TILE, CMID), jnp.float32)],
    )
    return pl.pallas_call(
        tile_kernel,
        grid_spec=grid_spec,
        out_shape=jax.ShapeDtypeStruct((size_x // 2, size_y // 2, size_z // 2 * COUT),
                                       jnp.bfloat16),
    )(
        flags,
        grown,
        band,
        indicator,
        gamma.reshape(1, CMID),
        beta.reshape(1, CMID),
        down,
        b_down.reshape(1, COUT),
    )


def solution(mesh):
    in_specs = (P("gx", "gy", None), P(None, "gy", None), P(), P(), P(), P(), P())
    out_specs = P("gx", "gy", None)
    return jax.shard_map(shards, mesh=mesh, in_specs=in_specs, out_specs=out_specs, check_vma=False)
```

```python
import jax
import jax.numpy as jnp
from jax import lax
from jax.experimental import pallas as pl
from jax.experimental.pallas import tpu as pltpu
from jax.sharding import PartitionSpec as P

CIN = 64
CMID = 128
COUT = 128
GROUPS = 8
TILE = 16
EPS = 1e-05


def neighbour(block, step_x, step_y):
    count_x, count_y = lax.axis_size("gx"), lax.axis_size("gy")
    pairs = []
    for ix in range(count_x):
        for iy in range(count_y):
            tx, ty = ix + step_x, iy + step_y
            if 0 <= tx < count_x and 0 <= ty < count_y:
                pairs.append((ix * count_y + iy, tx * count_y + ty))
    return lax.ppermute(block, ("gx", "gy"), pairs)


def halo_pieces(block):
    low_x = neighbour(block[-1], 1, 0)
    high_x = neighbour(block[0], -1, 0)
    column_hi = jnp.concatenate([low_x[None, -1], block[:, -1], high_x[None, -1]], axis=0)
    column_lo = jnp.concatenate([low_x[None, 0], block[:, 0], high_x[None, 0]], axis=0)
    low_y = neighbour(column_hi, 0, 1)
    high_y = neighbour(column_lo, 0, -1)
    return low_x, high_x, low_y, high_y


def build_band(w_conv):
    taps = w_conv.reshape(9, 3, CIN, CMID)
    zero = jnp.zeros((9, CIN, CMID), w_conv.dtype)
    first = jnp.concatenate([taps[:, 0], taps[:, 1], taps[:, 2], zero], axis=1)
    second = jnp.concatenate([zero, taps[:, 0], taps[:, 1], taps[:, 2]], axis=1)
    return jnp.concatenate([first, second], axis=2)


def group_sum(row, indicator):
    row = jnp.broadcast_to(row, (8, row.shape[1]))
    total = jnp.zeros(row.shape, jnp.float32)
    rest = row
    for _ in range(3):
        piece = rest.astype(jnp.bfloat16)
        total = total + jnp.dot(piece, indicator, preferred_element_type=jnp.float32)
        rest = rest - piece.astype(jnp.float32)
    return total[0:1]


def tile_kernel(tissue_ref, index_ref, volume_ref, low_x_ref, high_x_ref, low_y_ref,
                high_y_ref, band_ref, ind_ref, gamma_ref, beta_ref, down_ref, bias_ref, out_ref,
                grown_ref, conv_ref):
    pos_x, pos_y, pos_z = pl.program_id(0), pl.program_id(1), pl.program_id(2)
    tiles_x, tiles_z = pl.num_programs(0), pl.num_programs(2)
    flag = tissue_ref[index_ref[0] * tiles_x + pos_x, pos_y, pos_z]
    rows = TILE * TILE
    half = TILE // 2
    pairs = half + 1
    span = TILE * CIN
    pad = 2 * CIN
    start = pos_z * span
    size_x, size_y = volume_ref.shape[0], volume_ref.shape[1]

    @pl.when((pos_x == 0) & (pos_y == 0) & (pos_z == 0))
    def _():
        def place(row, carry):
            grown_ref[row + 1, 1:size_y + 1, :] = volume_ref[row]
            return carry

        lax.fori_loop(0, size_x, place, 0)
        grown_ref[0, 1:size_y + 1, :] = low_x_ref[...]
        grown_ref[size_x + 1, 1:size_y + 1, :] = high_x_ref[...]
        for row in range(size_x + 2):
            grown_ref[row, 0:1, :] = low_y_ref[row:row + 1, :]
            grown_ref[row, size_y + 1:size_y + 2, :] = high_y_ref[row:row + 1, :]

    def pair_conv(col, pair, offset, width, band_lo):
        lane_start = pl.multiple_of(start + offset, 128)
        acc = None
        for tap in range(9):
            shift_x, shift_y = tap // 3, tap % 3
            slab = grown_ref[pl.ds(pos_x * TILE + shift_x, TILE),
                             pl.ds(col * TILE + shift_y, TILE), pl.ds(lane_start, width)]
            part = jnp.dot(slab.reshape(rows, width), band_ref[tap, band_lo:band_lo + width, :],
                           preferred_element_type=jnp.float32)
            acc = part if acc is None else acc + part
        conv_ref[2 * pair] = acc[:, :CMID]
        conv_ref[2 * pair + 1] = acc[:, CMID:]

    def tile_conv(col):
        @pl.when(pos_z > 0)
        def _():
            pair_conv(col, 0, -pad, 2 * pad, 0)

        @pl.when(pos_z == 0)
        def _():
            pair_conv(col, 0, 0, pad, pad)

        for pair in range(1, pairs - 1):
            pair_conv(col, pair, pad * (pair - 1), 2 * pad, 0)

        @pl.when(pos_z < tiles_z - 1)
        def _():
            pair_conv(col, pairs - 1, pad * (pairs - 2), 2 * pad, 0)

        @pl.when(pos_z == tiles_z - 1)
        def _():
            pair_conv(col, pairs - 1, pad * (pairs - 2), pad, 0)

    @pl.when(flag > 0)
    def _():
        for col in range(grown_ref.shape[1] // TILE):
            @pl.when(pos_y == col)
            def _():
                tile_conv(col)

        count = float(rows * TILE * (CMID // GROUPS))
        indicator = ind_ref[...]
        total = jnp.zeros((1, CMID), jnp.float32)
        for depth in range(1, TILE + 1):
            total = total + jnp.sum(conv_ref[depth], axis=0, keepdims=True)
        mean = group_sum(total, indicator) / count
        total = jnp.zeros((1, CMID), jnp.float32)
        for depth in range(1, TILE + 1):
            diff = conv_ref[depth] - mean
            total = total + jnp.sum(diff * diff, axis=0, keepdims=True)
        var = group_sum(total, indicator) / count
        scale = lax.rsqrt(var + EPS) * gamma_ref[...]
        shift = beta_ref[...]

        results = [None] * half
        for pick_b in range(2):
            picked = conv_ref[:, pl.ds(pick_b, rows // 2, stride=2), :]
            normed = [
                jnp.maximum((picked[depth] - mean) * scale + shift, 0.0)
                .reshape(half, 2, half, CMID)
                for depth in range(1, TILE + 1)
            ]
            for pick_a in range(2):
                corners = [n[:, pick_a].reshape(half * half, CMID).astype(jnp.bfloat16)
                           for n in normed]
                lhs = jnp.concatenate([
                    jnp.concatenate([corners[2 * depth], corners[2 * depth + 1]], axis=1)
                    for depth in range(half)
                ], axis=0)
                part = jnp.dot(lhs, down_ref[pick_a * 2 + pick_b],
                               preferred_element_type=jnp.float32)
                for depth in range(half):
                    piece = part[half * half * depth:half * half * (depth + 1)]
                    results[depth] = piece if results[depth] is None else results[depth] + piece
        bias = bias_ref[...]
        merged = jnp.concatenate([r + bias for r in results], axis=1)
        out_ref[...] = merged.reshape(half, half, half * COUT).astype(jnp.bfloat16)

    @pl.when(flag == 0)
    def _():
        out_ref[...] = jnp.zeros(out_ref.shape, out_ref.dtype)


def shards(volume, tissue, w_conv, gamma, beta, w_down, b_down):
    own_index = lax.axis_index("gx")
    size_x, size_y, merged = volume.shape
    size_z = merged // CIN
    tiles_x, tiles_y, tiles_z = size_x // TILE, size_y // TILE, size_z // TILE
    half = TILE // 2
    low_x, high_x, low_y, high_y = halo_pieces(volume)
    band = build_band(w_conv)
    lane = jnp.arange(CMID, dtype=jnp.int32)
    group_size = CMID // GROUPS
    indicator = (lane[:, None] // group_size == lane[None, :] // group_size).astype(jnp.bfloat16)
    down = w_down.reshape(4, 2 * CMID, COUT)

    full = lambda shape: pl.BlockSpec(shape, lambda i, j, k, t, o: (0,) * len(shape))
    grid_spec = pltpu.PrefetchScalarGridSpec(
        num_scalar_prefetch=2,
        grid=(tiles_x, tiles_y, tiles_z),
        in_specs=[
            full(volume.shape),
            full(low_x.shape),
            full(high_x.shape),
            full(low_y.shape),
            full(high_y.shape),
            full((9, 4 * CIN, 2 * CMID)),
            full((CMID, CMID)),
            full((1, CMID)),
            full((1, CMID)),
            full((4, 2 * CMID, COUT)),
            full((1, COUT)),
        ],
        out_specs=pl.BlockSpec((half, half, half * COUT), lambda i, j, k, t, o: (i, j, k)),
        scratch_shapes=[
            pltpu.VMEM((size_x + 2, size_y + 2, merged), jnp.bfloat16),
            pltpu.VMEM((TILE + 2, TILE * TILE, CMID), jnp.float32),
        ],
    )
    return pl.pallas_call(
        tile_kernel,
        grid_spec=grid_spec,
        out_shape=jax.ShapeDtypeStruct((size_x // 2, size_y // 2, size_z // 2 * COUT),
                                       jnp.bfloat16),
    )(
        tissue.astype(jnp.int32),
        own_index.astype(jnp.int32).reshape(1),
        volume,
        low_x,
        high_x,
        low_y,
        high_y,
        band,
        indicator,
        gamma.reshape(1, CMID),
        beta.reshape(1, CMID),
        down,
        b_down.reshape(1, COUT),
    )


def solution(mesh):
    in_specs = (P("gx", "gy", None), P(None, "gy", None), P(), P(), P(), P(), P())
    out_specs = P("gx", "gy", None)
    return jax.shard_map(shards, mesh=mesh, in_specs=in_specs, out_specs=out_specs, check_vma=False)
```

```python
import jax
import jax.numpy as jnp
from jax import lax
from jax.experimental import pallas as pl
from jax.experimental.pallas import tpu as pltpu
from jax.sharding import PartitionSpec as P

CIN = 64
CMID = 128
COUT = 128
GROUPS = 8
TILE = 16
EPS = 1e-05


def neighbour(block, step_x, step_y):
    count_x, count_y = lax.axis_size("gx"), lax.axis_size("gy")
    pairs = []
    for ix in range(count_x):
        for iy in range(count_y):
            tx, ty = ix + step_x, iy + step_y
            if 0 <= tx < count_x and 0 <= ty < count_y:
                pairs.append((ix * count_y + iy, tx * count_y + ty))
    return lax.ppermute(block, ("gx", "gy"), pairs)


def halo_pieces(block):
    low_x = neighbour(block[-1], 1, 0)
    high_x = neighbour(block[0], -1, 0)
    column_hi = jnp.concatenate([low_x[None, -1], block[:, -1], high_x[None, -1]], axis=0)
    column_lo = jnp.concatenate([low_x[None, 0], block[:, 0], high_x[None, 0]], axis=0)
    low_y = neighbour(column_hi, 0, 1)
    high_y = neighbour(column_lo, 0, -1)
    return low_x, high_x, low_y, high_y


def build_band(w_conv):
    taps = w_conv.reshape(9, 3, CIN, CMID)
    zero = jnp.zeros((9, CIN, CMID), w_conv.dtype)
    first = jnp.concatenate([taps[:, 0], taps[:, 1], taps[:, 2], zero], axis=1)
    second = jnp.concatenate([zero, taps[:, 0], taps[:, 1], taps[:, 2]], axis=1)
    return jnp.concatenate([first, second], axis=2)


def group_sum(row, indicator):
    row = jnp.broadcast_to(row, (8, row.shape[1]))
    total = jnp.zeros(row.shape, jnp.float32)
    rest = row
    for _ in range(3):
        piece = rest.astype(jnp.bfloat16)
        total = total + jnp.dot(piece, indicator, preferred_element_type=jnp.float32)
        rest = rest - piece.astype(jnp.float32)
    return total[0:1]


def tile_kernel(flags_ref, volume_ref, low_x_ref, high_x_ref, low_y_ref, high_y_ref,
                band_ref, ind_ref, gamma_ref, beta_ref, down_ref, bias_ref, out_ref,
                grown_ref, conv_ref):
    pos_x, pos_y, pos_z = pl.program_id(0), pl.program_id(1), pl.program_id(2)
    tiles_y, tiles_z = pl.num_programs(1), pl.num_programs(2)
    flag = flags_ref[(pos_x * tiles_y + pos_y) * tiles_z + pos_z]
    rows = TILE * TILE
    half = TILE // 2
    span = TILE * CIN
    size_x, size_y, merged = volume_ref.shape
    start = pos_z * span

    @pl.when((pos_x == 0) & (pos_y == 0) & (pos_z == 0))
    def _():
        edge = jnp.zeros((size_x + 2, size_y + 2, CIN), grown_ref.dtype)
        grown_ref[:, :, 0:CIN] = edge
        grown_ref[:, :, CIN + merged:2 * CIN + merged] = edge

        def place(row, carry):
            grown_ref[row + 1, 1:size_y + 1, CIN:CIN + merged] = volume_ref[row]
            return carry

        lax.fori_loop(0, size_x, place, 0)
        grown_ref[0, 1:size_y + 1, CIN:CIN + merged] = low_x_ref[...]
        grown_ref[size_x + 1, 1:size_y + 1, CIN:CIN + merged] = high_x_ref[...]
        for row in range(size_x + 2):
            grown_ref[row, 0:1, CIN:CIN + merged] = low_y_ref[row:row + 1, :]
            grown_ref[row, size_y + 1:size_y + 2, CIN:CIN + merged] = high_y_ref[row:row + 1, :]

    def tile_conv(col):
        for pair in range(half):
            lane_start = pl.multiple_of(start + 2 * CIN * pair, 128)
            acc = None
            for tap in range(9):
                shift_x, shift_y = tap // 3, tap % 3
                slab = grown_ref[pl.ds(pos_x * TILE + shift_x, TILE),
                                 pl.ds(col * TILE + shift_y, TILE), pl.ds(lane_start, 4 * CIN)]
                part = jnp.dot(slab.reshape(rows, 4 * CIN), band_ref[tap],
                               preferred_element_type=jnp.float32)
                acc = part if acc is None else acc + part
            conv_ref[2 * pair] = acc[:, :CMID]
            conv_ref[2 * pair + 1] = acc[:, CMID:]

    @pl.when(flag > 0)
    def _():
        for col in range(size_y // TILE):
            @pl.when(pos_y == col)
            def _():
                tile_conv(col)

        count = float(rows * TILE * (CMID // GROUPS))
        indicator = ind_ref[...]
        total = jnp.zeros((1, CMID), jnp.float32)
        for depth in range(TILE):
            total = total + jnp.sum(conv_ref[depth], axis=0, keepdims=True)
        mean = group_sum(total, indicator) / count
        total = jnp.zeros((1, CMID), jnp.float32)
        for depth in range(TILE):
            diff = conv_ref[depth] - mean
            total = total + jnp.sum(diff * diff, axis=0, keepdims=True)
        var = group_sum(total, indicator) / count
        scale = lax.rsqrt(var + EPS) * gamma_ref[...]
        shift = beta_ref[...]

        results = [None] * half
        for pick_b in range(2):
            picked = conv_ref[:, pl.ds(pick_b, rows // 2, stride=2), :]
            normed = [
                jnp.maximum((picked[depth] - mean) * scale + shift, 0.0)
                .reshape(half, 2, half, CMID)
                for depth in range(TILE)
            ]
            for pick_a in range(2):
                corners = [n[:, pick_a].reshape(half * half, CMID).astype(jnp.bfloat16)
                           for n in normed]
                lhs = jnp.concatenate([
                    jnp.concatenate([corners[2 * depth], corners[2 * depth + 1]], axis=1)
                    for depth in range(half)
                ], axis=0)
                part = jnp.dot(lhs, down_ref[pick_a * 2 + pick_b],
                               preferred_element_type=jnp.float32)
                for depth in range(half):
                    piece = part[half * half * depth:half * half * (depth + 1)]
                    results[depth] = piece if results[depth] is None else results[depth] + piece
        bias = bias_ref[...]
        merged = jnp.concatenate([r + bias for r in results], axis=1)
        out_ref[...] = merged.reshape(half, half, half * COUT).astype(jnp.bfloat16)

    @pl.when(flag == 0)
    def _():
        out_ref[...] = jnp.zeros(out_ref.shape, out_ref.dtype)


def shards(volume, tissue, w_conv, gamma, beta, w_down, b_down):
    own_index = lax.axis_index("gx")
    size_x, size_y, merged = volume.shape
    size_z = merged // CIN
    tiles_x, tiles_y, tiles_z = size_x // TILE, size_y // TILE, size_z // TILE
    half = TILE // 2
    low_x, high_x, low_y, high_y = halo_pieces(volume)
    band = build_band(w_conv)
    lane = jnp.arange(CMID, dtype=jnp.int32)
    group_size = CMID // GROUPS
    indicator = (lane[:, None] // group_size == lane[None, :] // group_size).astype(jnp.bfloat16)
    down = w_down.reshape(4, 2 * CMID, COUT)
    own_tissue = lax.dynamic_slice_in_dim(tissue, own_index * tiles_x, tiles_x, 0)
    flags = own_tissue.reshape(tiles_x * tiles_y * tiles_z).astype(jnp.int32)

    full = lambda shape: pl.BlockSpec(shape, lambda i, j, k, f: (0,) * len(shape))
    grid_spec = pltpu.PrefetchScalarGridSpec(
        num_scalar_prefetch=1,
        grid=(tiles_x, tiles_y, tiles_z),
        in_specs=[
            full(volume.shape),
            full(low_x.shape),
            full(high_x.shape),
            full(low_y.shape),
            full(high_y.shape),
            full((9, 4 * CIN, 2 * CMID)),
            full((CMID, CMID)),
            full((1, CMID)),
            full((1, CMID)),
            full((4, 2 * CMID, COUT)),
            full((1, COUT)),
        ],
        out_specs=pl.BlockSpec((half, half, half * COUT), lambda i, j, k, f: (i, j, k)),
        scratch_shapes=[
            pltpu.VMEM((size_x + 2, size_y + 2, merged + 2 * CIN), jnp.bfloat16),
            pltpu.VMEM((TILE, TILE * TILE, CMID), jnp.float32),
        ],
    )
    return pl.pallas_call(
        tile_kernel,
        grid_spec=grid_spec,
        out_shape=jax.ShapeDtypeStruct((size_x // 2, size_y // 2, size_z // 2 * COUT),
                                       jnp.bfloat16),
    )(
        flags,
        volume,
        low_x,
        high_x,
        low_y,
        high_y,
        band,
        indicator,
        gamma.reshape(1, CMID),
        beta.reshape(1, CMID),
        down,
        b_down.reshape(1, COUT),
    )


def solution(mesh):
    in_specs = (P("gx", "gy", None), P(None, "gy", None), P(), P(), P(), P(), P())
    out_specs = P("gx", "gy", None)
    return jax.shard_map(shards, mesh=mesh, in_specs=in_specs, out_specs=out_specs, check_vma=False)
```

```python
import jax
import jax.numpy as jnp
from jax import lax
from jax.experimental import pallas as pl
from jax.experimental.pallas import tpu as pltpu
from jax.sharding import PartitionSpec as P

CIN = 64
CMID = 128
COUT = 128
GROUPS = 8
TILE = 16
EPS = 1e-05


def neighbour(block, step_x, step_y):
    count_x, count_y = lax.axis_size("gx"), lax.axis_size("gy")
    pairs = []
    for ix in range(count_x):
        for iy in range(count_y):
            tx, ty = ix + step_x, iy + step_y
            if 0 <= tx < count_x and 0 <= ty < count_y:
                pairs.append((ix * count_y + iy, tx * count_y + ty))
    return lax.ppermute(block, ("gx", "gy"), pairs)


def halo_pieces(block):
    low_x = neighbour(block[-1], 1, 0)
    high_x = neighbour(block[0], -1, 0)
    column_hi = jnp.concatenate([low_x[None, -1], block[:, -1], high_x[None, -1]], axis=0)
    column_lo = jnp.concatenate([low_x[None, 0], block[:, 0], high_x[None, 0]], axis=0)
    low_y = neighbour(column_hi, 0, 1)
    high_y = neighbour(column_lo, 0, -1)
    return low_x, high_x, low_y, high_y


def group_sum(row, indicator):
    row = jnp.broadcast_to(row, (8, row.shape[1]))
    total = jnp.zeros(row.shape, jnp.float32)
    rest = row
    for _ in range(3):
        piece = rest.astype(jnp.bfloat16)
        total = total + jnp.dot(piece, indicator, preferred_element_type=jnp.float32)
        rest = rest - piece.astype(jnp.float32)
    return total[0:1]


def tile_kernel(flags_ref, volume_ref, low_x_ref, high_x_ref, low_y_ref, high_y_ref,
                weight_ref, gamma_ref, beta_ref, down_ref, bias_ref, out_ref,
                grown_ref, conv_ref, band_ref):
    pos_x, pos_y, pos_z = pl.program_id(0), pl.program_id(1), pl.program_id(2)
    tiles_y, tiles_z = pl.num_programs(1), pl.num_programs(2)
    flag = flags_ref[(pos_x * tiles_y + pos_y) * tiles_z + pos_z]
    rows = TILE * TILE
    half = TILE // 2
    span = TILE * CIN
    size_x, size_y, merged = volume_ref.shape
    start = pos_z * span

    @pl.when((pos_x == 0) & (pos_y == 0) & (pos_z == 0))
    def _():
        edge = jnp.zeros((size_x + 2, size_y + 2, CIN), grown_ref.dtype)
        grown_ref[:, :, 0:CIN] = edge
        grown_ref[:, :, CIN + merged:2 * CIN + merged] = edge

        def place(row, carry):
            grown_ref[row + 1, 1:size_y + 1, CIN:CIN + merged] = volume_ref[row]
            return carry

        lax.fori_loop(0, size_x, place, 0)
        band_ref[...] = jnp.zeros(band_ref.shape, band_ref.dtype)
        for tap in range(9):
            for depth in range(3):
                taps = weight_ref[3 * tap + depth]
                band_ref[tap, CIN * depth:CIN * (depth + 1), 0:CMID] = taps
                band_ref[tap, CIN * (depth + 1):CIN * (depth + 2), CMID:2 * CMID] = taps
        grown_ref[0, 1:size_y + 1, CIN:CIN + merged] = low_x_ref[...]
        grown_ref[size_x + 1, 1:size_y + 1, CIN:CIN + merged] = high_x_ref[...]
        for row in range(size_x + 2):
            grown_ref[row, 0:1, CIN:CIN + merged] = low_y_ref[row:row + 1, :]
            grown_ref[row, size_y + 1:size_y + 2, CIN:CIN + merged] = high_y_ref[row:row + 1, :]

    def tile_conv(col):
        for pair in range(half):
            lane_start = pl.multiple_of(start + 2 * CIN * pair, 128)
            acc = None
            for tap in range(9):
                shift_x, shift_y = tap // 3, tap % 3
                slab = grown_ref[pl.ds(pos_x * TILE + shift_x, TILE),
                                 pl.ds(col * TILE + shift_y, TILE), pl.ds(lane_start, 4 * CIN)]
                part = jnp.dot(slab.reshape(rows, 4 * CIN), band_ref[tap],
                               preferred_element_type=jnp.float32)
                acc = part if acc is None else acc + part
            conv_ref[2 * pair] = acc[:, :CMID]
            conv_ref[2 * pair + 1] = acc[:, CMID:]

    @pl.when(flag > 0)
    def _():
        for col in range(size_y // TILE):
            @pl.when(pos_y == col)
            def _():
                tile_conv(col)

        count = float(rows * TILE * (CMID // GROUPS))
        lane_in = lax.broadcasted_iota(jnp.int32, (CMID, CMID), 0) // (CMID // GROUPS)
        lane_out = lax.broadcasted_iota(jnp.int32, (CMID, CMID), 1) // (CMID // GROUPS)
        indicator = (lane_in == lane_out).astype(jnp.bfloat16)
        total = jnp.zeros((1, CMID), jnp.float32)
        for depth in range(TILE):
            total = total + jnp.sum(conv_ref[depth], axis=0, keepdims=True)
        mean = group_sum(total, indicator) / count
        total = jnp.zeros((1, CMID), jnp.float32)
        for depth in range(TILE):
            diff = conv_ref[depth] - mean
            total = total + jnp.sum(diff * diff, axis=0, keepdims=True)
        var = group_sum(total, indicator) / count
        scale = lax.rsqrt(var + EPS) * gamma_ref[...]
        shift = beta_ref[...]

        results = [None] * half
        for pick_b in range(2):
            picked = conv_ref[:, pl.ds(pick_b, rows // 2, stride=2), :]
            normed = [
                jnp.maximum((picked[depth] - mean) * scale + shift, 0.0)
                .reshape(half, 2, half, CMID)
                for depth in range(TILE)
            ]
            for pick_a in range(2):
                corners = [n[:, pick_a].reshape(half * half, CMID).astype(jnp.bfloat16)
                           for n in normed]
                lhs = jnp.concatenate([
                    jnp.concatenate([corners[2 * depth], corners[2 * depth + 1]], axis=1)
                    for depth in range(half)
                ], axis=0)
                part = jnp.dot(lhs, down_ref[pick_a * 2 + pick_b],
                               preferred_element_type=jnp.float32)
                for depth in range(half):
                    piece = part[half * half * depth:half * half * (depth + 1)]
                    results[depth] = piece if results[depth] is None else results[depth] + piece
        bias = bias_ref[...]
        merged = jnp.concatenate([r + bias for r in results], axis=1)
        out_ref[...] = merged.reshape(half, half, half * COUT).astype(jnp.bfloat16)

    @pl.when(flag == 0)
    def _():
        out_ref[...] = jnp.zeros(out_ref.shape, out_ref.dtype)


def shards(volume, tissue, w_conv, gamma, beta, w_down, b_down):
    own_index = lax.axis_index("gx")
    size_x, size_y, merged = volume.shape
    size_z = merged // CIN
    tiles_x, tiles_y, tiles_z = size_x // TILE, size_y // TILE, size_z // TILE
    half = TILE // 2
    low_x, high_x, low_y, high_y = halo_pieces(volume)
    down = w_down.reshape(4, 2 * CMID, COUT)
    own_tissue = lax.dynamic_slice_in_dim(tissue, own_index * tiles_x, tiles_x, 0)
    flags = own_tissue.reshape(tiles_x * tiles_y * tiles_z).astype(jnp.int32)

    full = lambda shape: pl.BlockSpec(shape, lambda i, j, k, f: (0,) * len(shape))
    grid_spec = pltpu.PrefetchScalarGridSpec(
        num_scalar_prefetch=1,
        grid=(tiles_x, tiles_y, tiles_z),
        in_specs=[
            full(volume.shape),
            full(low_x.shape),
            full(high_x.shape),
            full(low_y.shape),
            full(high_y.shape),
            full((27, CIN, CMID)),
            full((1, CMID)),
            full((1, CMID)),
            full((4, 2 * CMID, COUT)),
            full((1, COUT)),
        ],
        out_specs=pl.BlockSpec((half, half, half * COUT), lambda i, j, k, f: (i, j, k)),
        scratch_shapes=[
            pltpu.VMEM((size_x + 2, size_y + 2, merged + 2 * CIN), jnp.bfloat16),
            pltpu.VMEM((TILE, TILE * TILE, CMID), jnp.float32),
            pltpu.VMEM((9, 4 * CIN, 2 * CMID), jnp.bfloat16),
        ],
    )
    return pl.pallas_call(
        tile_kernel,
        grid_spec=grid_spec,
        out_shape=jax.ShapeDtypeStruct((size_x // 2, size_y // 2, size_z // 2 * COUT),
                                       jnp.bfloat16),
    )(
        flags,
        volume,
        low_x,
        high_x,
        low_y,
        high_y,
        w_conv.reshape(27, CIN, CMID),
        gamma.reshape(1, CMID),
        beta.reshape(1, CMID),
        down,
        b_down.reshape(1, COUT),
    )


def solution(mesh):
    in_specs = (P("gx", "gy", None), P(None, "gy", None), P(), P(), P(), P(), P())
    out_specs = P("gx", "gy", None)
    return jax.shard_map(shards, mesh=mesh, in_specs=in_specs, out_specs=out_specs, check_vma=False)
```

```python
import jax
import jax.numpy as jnp
from jax import lax
from jax.experimental import pallas as pl
from jax.experimental.pallas import tpu as pltpu
from jax.sharding import PartitionSpec as P

CIN = 64
CMID = 128
COUT = 128
GROUPS = 8
TILE = 16
EPS = 1e-05


def neighbour(block, step_x, step_y):
    count_x, count_y = lax.axis_size("gx"), lax.axis_size("gy")
    pairs = []
    for ix in range(count_x):
        for iy in range(count_y):
            tx, ty = ix + step_x, iy + step_y
            if 0 <= tx < count_x and 0 <= ty < count_y:
                pairs.append((ix * count_y + iy, tx * count_y + ty))
    return lax.ppermute(block, ("gx", "gy"), pairs)


def halo_pieces(block):
    low_x = neighbour(block[-1], 1, 0)
    high_x = neighbour(block[0], -1, 0)
    column_hi = jnp.concatenate([low_x[None, -1], block[:, -1], high_x[None, -1]], axis=0)
    column_lo = jnp.concatenate([low_x[None, 0], block[:, 0], high_x[None, 0]], axis=0)
    low_y = neighbour(column_hi, 0, 1)
    high_y = neighbour(column_lo, 0, -1)
    return low_x, high_x, low_y, high_y


def group_sum(row, indicator):
    row = jnp.broadcast_to(row, (8, row.shape[1]))
    total = jnp.zeros(row.shape, jnp.float32)
    rest = row
    for _ in range(3):
        piece = rest.astype(jnp.bfloat16)
        total = total + jnp.dot(piece, indicator, preferred_element_type=jnp.float32)
        rest = rest - piece.astype(jnp.float32)
    return total[0:1]


def tile_kernel(flags_ref, volume_ref, low_x_ref, high_x_ref, low_y_ref, high_y_ref,
                weight_ref, gamma_ref, beta_ref, down_ref, bias_ref, out_ref,
                grown_ref, conv_ref, band_ref, sum_ref):
    pos_x, pos_y, pos_z = pl.program_id(0), pl.program_id(1), pl.program_id(2)
    tiles_y, tiles_z = pl.num_programs(1), pl.num_programs(2)
    flag = flags_ref[(pos_x * tiles_y + pos_y) * tiles_z + pos_z]
    rows = TILE * TILE
    half = TILE // 2
    span = TILE * CIN
    size_x, size_y, merged = volume_ref.shape
    start = pos_z * span

    @pl.when((pos_x == 0) & (pos_y == 0) & (pos_z == 0))
    def _():
        edge = jnp.zeros((size_x + 2, grown_ref.shape[1], CIN), grown_ref.dtype)
        grown_ref[:, :, 0:CIN] = edge
        grown_ref[:, :, CIN + merged:2 * CIN + merged] = edge

        def place(row, carry):
            grown_ref[row + 1, TILE:TILE + size_y, CIN:CIN + merged] = volume_ref[row]
            return carry

        lax.fori_loop(0, size_x, place, 0)
        grown_ref[0, TILE:TILE + size_y, CIN:CIN + merged] = low_x_ref[...]
        grown_ref[size_x + 1, TILE:TILE + size_y, CIN:CIN + merged] = high_x_ref[...]
        for row in range(size_x + 2):
            grown_ref[row, TILE - 1:TILE, CIN:CIN + merged] = low_y_ref[row:row + 1, :]
            grown_ref[row, TILE + size_y:TILE + size_y + 1, CIN:CIN + merged] = (
                high_y_ref[row:row + 1, :])
        band_ref[...] = jnp.zeros(band_ref.shape, band_ref.dtype)
        for tap in range(9):
            for depth in range(3):
                taps = weight_ref[3 * tap + depth]
                band_ref[tap, CIN * depth:CIN * (depth + 1), 0:CMID] = taps
                band_ref[tap, CIN * (depth + 1):CIN * (depth + 2), CMID:2 * CMID] = taps

    def tile_conv(col):
        total = None
        for pair in range(half):
            lane_start = pl.multiple_of(start + 2 * CIN * pair, 128)
            acc = None
            for tap in range(9):
                shift_x, shift_y = tap // 3, tap % 3
                slab = grown_ref[pl.ds(pos_x * TILE + shift_x, TILE),
                                 pl.ds(col * TILE + shift_y + TILE - 1, TILE),
                                 pl.ds(lane_start, 4 * CIN)]
                part = jnp.dot(slab.reshape(rows, 4 * CIN), band_ref[tap],
                               preferred_element_type=jnp.float32)
                acc = part if acc is None else acc + part
            conv_ref[2 * pair] = acc[:, :CMID]
            conv_ref[2 * pair + 1] = acc[:, CMID:]
            column = jnp.sum(acc, axis=0, keepdims=True)
            total = column if total is None else total + column
        sum_ref[...] = total[:, :CMID] + total[:, CMID:]

    @pl.when(flag > 0)
    def _():
        for col in range(size_y // TILE):
            @pl.when(pos_y == col)
            def _():
                tile_conv(col)

        count = float(rows * TILE * (CMID // GROUPS))
        lane_in = lax.broadcasted_iota(jnp.int32, (CMID, CMID), 0) // (CMID // GROUPS)
        lane_out = lax.broadcasted_iota(jnp.int32, (CMID, CMID), 1) // (CMID // GROUPS)
        indicator = (lane_in == lane_out).astype(jnp.bfloat16)
        mean = group_sum(sum_ref[...], indicator) / count
        total = jnp.zeros((1, CMID), jnp.float32)
        for depth in range(TILE):
            diff = conv_ref[depth] - mean
            total = total + jnp.sum(diff * diff, axis=0, keepdims=True)
        var = group_sum(total, indicator) / count
        scale = lax.rsqrt(var + EPS) * gamma_ref[...]
        shift = beta_ref[...]

        results = [None] * half
        for pick_b in range(2):
            picked = conv_ref[:, pl.ds(pick_b, rows // 2, stride=2), :]
            normed = [
                jnp.maximum((picked[depth] - mean) * scale + shift, 0.0)
                .reshape(half, 2, half, CMID)
                for depth in range(TILE)
            ]
            for pick_a in range(2):
                corners = [n[:, pick_a].reshape(half * half, CMID).astype(jnp.bfloat16)
                           for n in normed]
                lhs = jnp.concatenate([
                    jnp.concatenate([corners[2 * depth], corners[2 * depth + 1]], axis=1)
                    for depth in range(half)
                ], axis=0)
                part = jnp.dot(lhs, down_ref[pick_a * 2 + pick_b],
                               preferred_element_type=jnp.float32)
                for depth in range(half):
                    piece = part[half * half * depth:half * half * (depth + 1)]
                    results[depth] = piece if results[depth] is None else results[depth] + piece
        bias = bias_ref[...]
        merged = jnp.concatenate([r + bias for r in results], axis=1)
        out_ref[...] = merged.reshape(half, half, half * COUT).astype(jnp.bfloat16)

    @pl.when(flag == 0)
    def _():
        out_ref[...] = jnp.zeros(out_ref.shape, out_ref.dtype)


def shards(volume, tissue, w_conv, gamma, beta, w_down, b_down):
    own_index = lax.axis_index("gx")
    size_x, size_y, merged = volume.shape
    size_z = merged // CIN
    tiles_x, tiles_y, tiles_z = size_x // TILE, size_y // TILE, size_z // TILE
    half = TILE // 2
    low_x, high_x, low_y, high_y = halo_pieces(volume)
    down = w_down.reshape(4, 2 * CMID, COUT)
    own_tissue = lax.dynamic_slice_in_dim(tissue, own_index * tiles_x, tiles_x, 0)
    flags = own_tissue.reshape(tiles_x * tiles_y * tiles_z).astype(jnp.int32)

    full = lambda shape: pl.BlockSpec(shape, lambda i, j, k, f: (0,) * len(shape))
    grid_spec = pltpu.PrefetchScalarGridSpec(
        num_scalar_prefetch=1,
        grid=(tiles_x, tiles_y, tiles_z),
        in_specs=[
            full(volume.shape),
            full(low_x.shape),
            full(high_x.shape),
            full(low_y.shape),
            full(high_y.shape),
            full((27, CIN, CMID)),
            full((1, CMID)),
            full((1, CMID)),
            full((4, 2 * CMID, COUT)),
            full((1, COUT)),
        ],
        out_specs=pl.BlockSpec((half, half, half * COUT), lambda i, j, k, f: (i, j, k)),
        scratch_shapes=[
            pltpu.VMEM((size_x + 2, size_y + 2 * TILE, merged + 2 * CIN), jnp.bfloat16),
            pltpu.VMEM((TILE, TILE * TILE, CMID), jnp.float32),
            pltpu.VMEM((9, 4 * CIN, 2 * CMID), jnp.bfloat16),
            pltpu.VMEM((1, CMID), jnp.float32),
        ],
    )
    return pl.pallas_call(
        tile_kernel,
        grid_spec=grid_spec,
        out_shape=jax.ShapeDtypeStruct((size_x // 2, size_y // 2, size_z // 2 * COUT),
                                       jnp.bfloat16),
    )(
        flags,
        volume,
        low_x,
        high_x,
        low_y,
        high_y,
        w_conv.reshape(27, CIN, CMID),
        gamma.reshape(1, CMID),
        beta.reshape(1, CMID),
        down,
        b_down.reshape(1, COUT),
    )


def solution(mesh):
    in_specs = (P("gx", "gy", None), P(None, "gy", None), P(), P(), P(), P(), P())
    out_specs = P("gx", "gy", None)
    return jax.shard_map(shards, mesh=mesh, in_specs=in_specs, out_specs=out_specs, check_vma=False)
```

```python
import jax
import jax.numpy as jnp
from jax import lax
from jax.experimental import pallas as pl
from jax.experimental.pallas import tpu as pltpu
from jax.sharding import PartitionSpec as P

CIN = 64
CMID = 128
COUT = 128
GROUPS = 8
TILE = 16
EPS = 1e-05


def neighbour(block, step_x, step_y):
    count_x, count_y = lax.axis_size("gx"), lax.axis_size("gy")
    pairs = []
    for ix in range(count_x):
        for iy in range(count_y):
            tx, ty = ix + step_x, iy + step_y
            if 0 <= tx < count_x and 0 <= ty < count_y:
                pairs.append((ix * count_y + iy, tx * count_y + ty))
    return lax.ppermute(block, ("gx", "gy"), pairs)


def halo_pieces(block):
    low_x = neighbour(block[-1], 1, 0)
    high_x = neighbour(block[0], -1, 0)
    column_hi = jnp.concatenate([low_x[None, -1], block[:, -1], high_x[None, -1]], axis=0)
    column_lo = jnp.concatenate([low_x[None, 0], block[:, 0], high_x[None, 0]], axis=0)
    low_y = neighbour(column_hi, 0, 1)
    high_y = neighbour(column_lo, 0, -1)
    return low_x, high_x, low_y, high_y


def group_sum(row, indicator):
    row = jnp.broadcast_to(row, (8, row.shape[1]))
    total = jnp.zeros(row.shape, jnp.float32)
    rest = row
    for _ in range(3):
        piece = rest.astype(jnp.bfloat16)
        total = total + jnp.dot(piece, indicator, preferred_element_type=jnp.float32)
        rest = rest - piece.astype(jnp.float32)
    return total[0:1]


def tile_kernel(flags_ref, volume_ref, low_x_ref, high_x_ref, low_y_ref, high_y_ref,
                weight_ref, gamma_ref, beta_ref, down_ref, bias_ref, out_ref,
                grown_ref, conv_ref, band_ref, stat_ref):
    pos_x, pos_y, pos_z = pl.program_id(0), pl.program_id(1), pl.program_id(2)
    tiles_y, tiles_z = pl.num_programs(1), pl.num_programs(2)
    flag = flags_ref[(pos_x * tiles_y + pos_y) * tiles_z + pos_z]
    rows = TILE * TILE
    half = TILE // 2
    span = TILE * CIN
    size_x, size_y, merged = volume_ref.shape
    start = pos_z * span

    @pl.when((pos_x == 0) & (pos_y == 0) & (pos_z == 0))
    def _():
        edge = jnp.zeros((size_x + 2, grown_ref.shape[1], CIN), grown_ref.dtype)
        grown_ref[:, :, 0:CIN] = edge
        grown_ref[:, :, CIN + merged:2 * CIN + merged] = edge

        def place(row, carry):
            grown_ref[row + 1, TILE:TILE + size_y, CIN:CIN + merged] = volume_ref[row]
            return carry

        lax.fori_loop(0, size_x, place, 0)
        grown_ref[0, TILE:TILE + size_y, CIN:CIN + merged] = low_x_ref[...]
        grown_ref[size_x + 1, TILE:TILE + size_y, CIN:CIN + merged] = high_x_ref[...]
        for row in range(size_x + 2):
            grown_ref[row, TILE - 1:TILE, CIN:CIN + merged] = low_y_ref[row:row + 1, :]
            grown_ref[row, TILE + size_y:TILE + size_y + 1, CIN:CIN + merged] = (
                high_y_ref[row:row + 1, :])
        band_ref[...] = jnp.zeros(band_ref.shape, band_ref.dtype)
        for tap in range(9):
            for depth in range(3):
                taps = weight_ref[3 * tap + depth]
                band_ref[tap, CIN * depth:CIN * (depth + 1), 0:CMID] = taps
                band_ref[tap, CIN * (depth + 1):CIN * (depth + 2), CMID:2 * CMID] = taps

    def tile_conv(col):
        for pair in range(half):
            lane_start = pl.multiple_of(start + 2 * CIN * pair, 128)
            acc = None
            for tap in range(9):
                shift_x, shift_y = tap // 3, tap % 3
                slab = grown_ref[pl.ds(pos_x * TILE + shift_x, TILE),
                                 pl.ds(col * TILE + shift_y + TILE - 1, TILE),
                                 pl.ds(lane_start, 4 * CIN)]
                part = jnp.dot(slab.reshape(rows, 4 * CIN), band_ref[tap],
                               preferred_element_type=jnp.float32)
                acc = part if acc is None else acc + part
            conv_ref[2 * pair] = acc[:, :CMID]
            conv_ref[2 * pair + 1] = acc[:, CMID:]
            column = jnp.sum(acc, axis=0, keepdims=True)
            diff = acc - column / float(rows)
            spread = jnp.sum(diff * diff, axis=0, keepdims=True)
            stat_ref[2 * pair:2 * pair + 1, :] = column[:, :CMID]
            stat_ref[2 * pair + 1:2 * pair + 2, :] = column[:, CMID:]
            stat_ref[TILE + 2 * pair:TILE + 2 * pair + 1, :] = spread[:, :CMID]
            stat_ref[TILE + 2 * pair + 1:TILE + 2 * pair + 2, :] = spread[:, CMID:]

    @pl.when(flag > 0)
    def _():
        for col in range(size_y // TILE):
            @pl.when(pos_y == col)
            def _():
                tile_conv(col)

        count = float(rows * TILE * (CMID // GROUPS))
        lane_in = lax.broadcasted_iota(jnp.int32, (CMID, CMID), 0) // (CMID // GROUPS)
        lane_out = lax.broadcasted_iota(jnp.int32, (CMID, CMID), 1) // (CMID // GROUPS)
        indicator = (lane_in == lane_out).astype(jnp.bfloat16)
        sums = stat_ref[0:TILE, :]
        mean = group_sum(jnp.sum(sums, axis=0, keepdims=True), indicator) / count
        offset = sums / float(rows) - mean
        spread = jnp.sum(stat_ref[TILE:2 * TILE, :] + float(rows) * (offset * offset), axis=0,
                         keepdims=True)
        var = group_sum(spread, indicator) / count
        scale = lax.rsqrt(var + EPS) * gamma_ref[...]
        shift = beta_ref[...]

        results = [None] * half
        for pick_b in range(2):
            picked = conv_ref[:, pl.ds(pick_b, rows // 2, stride=2), :]
            normed = [
                jnp.maximum((picked[depth] - mean) * scale + shift, 0.0)
                .reshape(half, 2, half, CMID)
                for depth in range(TILE)
            ]
            for pick_a in range(2):
                corners = [n[:, pick_a].reshape(half * half, CMID).astype(jnp.bfloat16)
                           for n in normed]
                lhs = jnp.concatenate([
                    jnp.concatenate([corners[2 * depth], corners[2 * depth + 1]], axis=1)
                    for depth in range(half)
                ], axis=0)
                part = jnp.dot(lhs, down_ref[pick_a * 2 + pick_b],
                               preferred_element_type=jnp.float32)
                for depth in range(half):
                    piece = part[half * half * depth:half * half * (depth + 1)]
                    results[depth] = piece if results[depth] is None else results[depth] + piece
        bias = bias_ref[...]
        merged = jnp.concatenate([r + bias for r in results], axis=1)
        out_ref[...] = merged.reshape(half, half, half * COUT).astype(jnp.bfloat16)

    @pl.when(flag == 0)
    def _():
        out_ref[...] = jnp.zeros(out_ref.shape, out_ref.dtype)


def shards(volume, tissue, w_conv, gamma, beta, w_down, b_down):
    own_index = lax.axis_index("gx")
    size_x, size_y, merged = volume.shape
    size_z = merged // CIN
    tiles_x, tiles_y, tiles_z = size_x // TILE, size_y // TILE, size_z // TILE
    half = TILE // 2
    low_x, high_x, low_y, high_y = halo_pieces(volume)
    down = w_down.reshape(4, 2 * CMID, COUT)
    own_tissue = lax.dynamic_slice_in_dim(tissue, own_index * tiles_x, tiles_x, 0)
    flags = own_tissue.reshape(tiles_x * tiles_y * tiles_z).astype(jnp.int32)

    full = lambda shape: pl.BlockSpec(shape, lambda i, j, k, f: (0,) * len(shape))
    grid_spec = pltpu.PrefetchScalarGridSpec(
        num_scalar_prefetch=1,
        grid=(tiles_x, tiles_y, tiles_z),
        in_specs=[
            full(volume.shape),
            full(low_x.shape),
            full(high_x.shape),
            full(low_y.shape),
            full(high_y.shape),
            full((27, CIN, CMID)),
            full((1, CMID)),
            full((1, CMID)),
            full((4, 2 * CMID, COUT)),
            full((1, COUT)),
        ],
        out_specs=pl.BlockSpec((half, half, half * COUT), lambda i, j, k, f: (i, j, k)),
        scratch_shapes=[
            pltpu.VMEM((size_x + 2, size_y + 2 * TILE, merged + 2 * CIN), jnp.bfloat16),
            pltpu.VMEM((TILE, TILE * TILE, CMID), jnp.float32),
            pltpu.VMEM((9, 4 * CIN, 2 * CMID), jnp.bfloat16),
            pltpu.VMEM((2 * TILE, CMID), jnp.float32),
        ],
    )
    return pl.pallas_call(
        tile_kernel,
        grid_spec=grid_spec,
        out_shape=jax.ShapeDtypeStruct((size_x // 2, size_y // 2, size_z // 2 * COUT),
                                       jnp.bfloat16),
    )(
        flags,
        volume,
        low_x,
        high_x,
        low_y,
        high_y,
        w_conv.reshape(27, CIN, CMID),
        gamma.reshape(1, CMID),
        beta.reshape(1, CMID),
        down,
        b_down.reshape(1, COUT),
    )


def solution(mesh):
    in_specs = (P("gx", "gy", None), P(None, "gy", None), P(), P(), P(), P(), P())
    out_specs = P("gx", "gy", None)
    return jax.shard_map(shards, mesh=mesh, in_specs=in_specs, out_specs=out_specs, check_vma=False)
```

```python
import jax
import jax.numpy as jnp
from jax import lax
from jax.experimental import pallas as pl
from jax.experimental.pallas import tpu as pltpu
from jax.sharding import PartitionSpec as P

CIN = 64
CMID = 128
COUT = 128
GROUPS = 8
TILE = 16
EPS = 1e-05


def neighbour(block, step_x, step_y):
    count_x, count_y = lax.axis_size("gx"), lax.axis_size("gy")
    pairs = []
    for ix in range(count_x):
        for iy in range(count_y):
            tx, ty = ix + step_x, iy + step_y
            if 0 <= tx < count_x and 0 <= ty < count_y:
                pairs.append((ix * count_y + iy, tx * count_y + ty))
    return lax.ppermute(block, ("gx", "gy"), pairs)


def halo_pieces(block):
    low_x = neighbour(block[-1], 1, 0)
    high_x = neighbour(block[0], -1, 0)
    low_y = neighbour(block[:, -1], 0, 1)
    high_y = neighbour(block[:, 0], 0, -1)
    corner_low = neighbour(jnp.stack([low_x[-1], high_x[-1]]), 0, 1)
    corner_high = neighbour(jnp.stack([low_x[0], high_x[0]]), 0, -1)
    low_y = jnp.concatenate([corner_low[0:1], low_y, corner_low[1:2]], axis=0)
    high_y = jnp.concatenate([corner_high[0:1], high_y, corner_high[1:2]], axis=0)
    return low_x, high_x, low_y, high_y


def group_sum(row, indicator):
    row = jnp.broadcast_to(row, (8, row.shape[1]))
    total = jnp.zeros(row.shape, jnp.float32)
    rest = row
    for _ in range(3):
        piece = rest.astype(jnp.bfloat16)
        total = total + jnp.dot(piece, indicator, preferred_element_type=jnp.float32)
        rest = rest - piece.astype(jnp.float32)
    return total[0:1]


def tile_kernel(flags_ref, volume_ref, low_x_ref, high_x_ref, low_y_ref, high_y_ref,
                weight_ref, gamma_ref, beta_ref, down_ref, bias_ref, out_ref,
                grown_ref, conv_ref, band_ref, sum_ref):
    pos_x, pos_y, pos_z = pl.program_id(0), pl.program_id(1), pl.program_id(2)
    tiles_y, tiles_z = pl.num_programs(1), pl.num_programs(2)
    flag = flags_ref[(pos_x * tiles_y + pos_y) * tiles_z + pos_z]
    rows = TILE * TILE
    half = TILE // 2
    span = TILE * CIN
    size_x, size_y, merged = volume_ref.shape
    start = pos_z * span

    @pl.when((pos_x == 0) & (pos_y == 0) & (pos_z == 0))
    def _():
        edge = jnp.zeros((size_x + 2, grown_ref.shape[1], CIN), grown_ref.dtype)
        grown_ref[:, :, 0:CIN] = edge
        grown_ref[:, :, CIN + merged:2 * CIN + merged] = edge

        def place(row, carry):
            grown_ref[row + 1, TILE:TILE + size_y, CIN:CIN + merged] = volume_ref[row]
            return carry

        lax.fori_loop(0, size_x, place, 0)
        grown_ref[0, TILE:TILE + size_y, CIN:CIN + merged] = low_x_ref[...]
        grown_ref[size_x + 1, TILE:TILE + size_y, CIN:CIN + merged] = high_x_ref[...]
        for row in range(size_x + 2):
            grown_ref[row, TILE - 1:TILE, CIN:CIN + merged] = low_y_ref[row:row + 1, :]
            grown_ref[row, TILE + size_y:TILE + size_y + 1, CIN:CIN + merged] = (
                high_y_ref[row:row + 1, :])
        band_ref[...] = jnp.zeros(band_ref.shape, band_ref.dtype)
        for tap in range(9):
            for depth in range(3):
                taps = weight_ref[3 * tap + depth]
                band_ref[tap, CIN * depth:CIN * (depth + 1), 0:CMID] = taps
                band_ref[tap, CIN * (depth + 1):CIN * (depth + 2), CMID:2 * CMID] = taps

    def tile_conv(col):
        total = None
        for pair in range(half):
            lane_start = pl.multiple_of(start + 2 * CIN * pair, 128)
            acc = None
            for tap in range(9):
                shift_x, shift_y = tap // 3, tap % 3
                slab = grown_ref[pl.ds(pos_x * TILE + shift_x, TILE),
                                 pl.ds(col * TILE + shift_y + TILE - 1, TILE),
                                 pl.ds(lane_start, 4 * CIN)]
                part = jnp.dot(slab.reshape(rows, 4 * CIN), band_ref[tap],
                               preferred_element_type=jnp.float32)
                acc = part if acc is None else acc + part
            conv_ref[2 * pair] = acc[:, :CMID]
            conv_ref[2 * pair + 1] = acc[:, CMID:]
            column = jnp.sum(acc, axis=0, keepdims=True)
            total = column if total is None else total + column
        sum_ref[...] = total[:, :CMID] + total[:, CMID:]

    @pl.when(flag > 0)
    def _():
        for col in range(size_y // TILE):
            @pl.when(pos_y == col)
            def _():
                tile_conv(col)

        count = float(rows * TILE * (CMID // GROUPS))
        lane_in = lax.broadcasted_iota(jnp.int32, (CMID, CMID), 0) // (CMID // GROUPS)
        lane_out = lax.broadcasted_iota(jnp.int32, (CMID, CMID), 1) // (CMID // GROUPS)
        indicator = (lane_in == lane_out).astype(jnp.bfloat16)
        mean = group_sum(sum_ref[...], indicator) / count
        total = jnp.zeros((1, CMID), jnp.float32)
        for depth in range(TILE):
            diff = conv_ref[depth] - mean
            total = total + jnp.sum(diff * diff, axis=0, keepdims=True)
        var = group_sum(total, indicator) / count
        scale = lax.rsqrt(var + EPS) * gamma_ref[...]
        shift = beta_ref[...]

        results = [None] * half
        for pick_b in range(2):
            picked = conv_ref[:, pl.ds(pick_b, rows // 2, stride=2), :]
            normed = [
                jnp.maximum((picked[depth] - mean) * scale + shift, 0.0)
                .reshape(half, 2, half, CMID)
                for depth in range(TILE)
            ]
            for pick_a in range(2):
                corners = [n[:, pick_a].reshape(half * half, CMID).astype(jnp.bfloat16)
                           for n in normed]
                lhs = jnp.concatenate([
                    jnp.concatenate([corners[2 * depth], corners[2 * depth + 1]], axis=1)
                    for depth in range(half)
                ], axis=0)
                part = jnp.dot(lhs, down_ref[pick_a * 2 + pick_b],
                               preferred_element_type=jnp.float32)
                for depth in range(half):
                    piece = part[half * half * depth:half * half * (depth + 1)]
                    results[depth] = piece if results[depth] is None else results[depth] + piece
        bias = bias_ref[...]
        merged = jnp.concatenate([r + bias for r in results], axis=1)
        out_ref[...] = merged.reshape(half, half, half * COUT).astype(jnp.bfloat16)

    @pl.when(flag == 0)
    def _():
        out_ref[...] = jnp.zeros(out_ref.shape, out_ref.dtype)


def shards(volume, tissue, w_conv, gamma, beta, w_down, b_down):
    own_index = lax.axis_index("gx")
    size_x, size_y, merged = volume.shape
    size_z = merged // CIN
    tiles_x, tiles_y, tiles_z = size_x // TILE, size_y // TILE, size_z // TILE
    half = TILE // 2
    low_x, high_x, low_y, high_y = halo_pieces(volume)
    down = w_down.reshape(4, 2 * CMID, COUT)
    own_tissue = lax.dynamic_slice_in_dim(tissue, own_index * tiles_x, tiles_x, 0)
    flags = own_tissue.reshape(tiles_x * tiles_y * tiles_z).astype(jnp.int32)

    full = lambda shape: pl.BlockSpec(shape, lambda i, j, k, f: (0,) * len(shape))
    grid_spec = pltpu.PrefetchScalarGridSpec(
        num_scalar_prefetch=1,
        grid=(tiles_x, tiles_y, tiles_z),
        in_specs=[
            full(volume.shape),
            full(low_x.shape),
            full(high_x.shape),
            full(low_y.shape),
            full(high_y.shape),
            full((27, CIN, CMID)),
            full((1, CMID)),
            full((1, CMID)),
            full((4, 2 * CMID, COUT)),
            full((1, COUT)),
        ],
        out_specs=pl.BlockSpec((half, half, half * COUT), lambda i, j, k, f: (i, j, k)),
        scratch_shapes=[
            pltpu.VMEM((size_x + 2, size_y + 2 * TILE, merged + 2 * CIN), jnp.bfloat16),
            pltpu.VMEM((TILE, TILE * TILE, CMID), jnp.float32),
            pltpu.VMEM((9, 4 * CIN, 2 * CMID), jnp.bfloat16),
            pltpu.VMEM((1, CMID), jnp.float32),
        ],
    )
    return pl.pallas_call(
        tile_kernel,
        grid_spec=grid_spec,
        out_shape=jax.ShapeDtypeStruct((size_x // 2, size_y // 2, size_z // 2 * COUT),
                                       jnp.bfloat16),
    )(
        flags,
        volume,
        low_x,
        high_x,
        low_y,
        high_y,
        w_conv.reshape(27, CIN, CMID),
        gamma.reshape(1, CMID),
        beta.reshape(1, CMID),
        down,
        b_down.reshape(1, COUT),
    )


def solution(mesh):
    in_specs = (P("gx", "gy", None), P(None, "gy", None), P(), P(), P(), P(), P())
    out_specs = P("gx", "gy", None)
    return jax.shard_map(shards, mesh=mesh, in_specs=in_specs, out_specs=out_specs, check_vma=False)
```

```python
import jax
import jax.numpy as jnp
from jax import lax
from jax.experimental import pallas as pl
from jax.experimental.pallas import tpu as pltpu
from jax.sharding import PartitionSpec as P

CIN = 64
CMID = 128
COUT = 128
GROUPS = 8
TILE = 16
EPS = 1e-05


def neighbour(block, step_x, step_y):
    count_x, count_y = lax.axis_size("gx"), lax.axis_size("gy")
    pairs = []
    for ix in range(count_x):
        for iy in range(count_y):
            tx, ty = ix + step_x, iy + step_y
            if 0 <= tx < count_x and 0 <= ty < count_y:
                pairs.append((ix * count_y + iy, tx * count_y + ty))
    return lax.ppermute(block, ("gx", "gy"), pairs)


def halo_pieces(block):
    low_x = neighbour(block[-1], 1, 0)
    high_x = neighbour(block[0], -1, 0)
    column_hi = jnp.concatenate([low_x[None, -1], block[:, -1], high_x[None, -1]], axis=0)
    column_lo = jnp.concatenate([low_x[None, 0], block[:, 0], high_x[None, 0]], axis=0)
    low_y = neighbour(column_hi, 0, 1)
    high_y = neighbour(column_lo, 0, -1)
    return low_x, high_x, low_y, high_y


def group_sum(row, indicator):
    row = jnp.broadcast_to(row, (8, row.shape[1]))
    total = jnp.zeros(row.shape, jnp.float32)
    rest = row
    for _ in range(3):
        piece = rest.astype(jnp.bfloat16)
        total = total + jnp.dot(piece, indicator, preferred_element_type=jnp.float32)
        rest = rest - piece.astype(jnp.float32)
    return total[0:1]


def tile_kernel(flags_ref, volume_ref, low_x_ref, high_x_ref, low_y_ref, high_y_ref,
                weight_ref, gamma_ref, beta_ref, down_ref, bias_ref, out_ref,
                grown_ref, conv_ref, band_ref, sum_ref):
    pos_x, pos_y = pl.program_id(0), pl.program_id(1)
    tiles_y = pl.num_programs(1)
    rows = TILE * TILE
    half = TILE // 2
    span = TILE * CIN
    size_x, size_y, merged = volume_ref.shape
    tiles_z = merged // span

    @pl.when((pos_x == 0) & (pos_y == 0))
    def _():
        edge = jnp.zeros((size_x + 2, grown_ref.shape[1], CIN), grown_ref.dtype)
        grown_ref[:, :, 0:CIN] = edge
        grown_ref[:, :, CIN + merged:2 * CIN + merged] = edge

        def place(row, carry):
            grown_ref[row + 1, TILE:TILE + size_y, CIN:CIN + merged] = volume_ref[row]
            return carry

        lax.fori_loop(0, size_x, place, 0)
        grown_ref[0, TILE:TILE + size_y, CIN:CIN + merged] = low_x_ref[...]
        grown_ref[size_x + 1, TILE:TILE + size_y, CIN:CIN + merged] = high_x_ref[...]
        for row in range(size_x + 2):
            grown_ref[row, TILE - 1:TILE, CIN:CIN + merged] = low_y_ref[row:row + 1, :]
            grown_ref[row, TILE + size_y:TILE + size_y + 1, CIN:CIN + merged] = (
                high_y_ref[row:row + 1, :])
        band_ref[...] = jnp.zeros(band_ref.shape, band_ref.dtype)
        for tap in range(9):
            for depth in range(3):
                taps = weight_ref[3 * tap + depth]
                band_ref[tap, CIN * depth:CIN * (depth + 1), 0:CMID] = taps
                band_ref[tap, CIN * (depth + 1):CIN * (depth + 2), CMID:2 * CMID] = taps

    def tile_conv(col, start):
        total = None
        for pair in range(half):
            lane_start = start + 2 * CIN * pair
            acc = None
            for tap in range(9):
                shift_x, shift_y = tap // 3, tap % 3
                slab = grown_ref[pl.ds(pos_x * TILE + shift_x, TILE),
                                 pl.ds(col * TILE + shift_y + TILE - 1, TILE),
                                 pl.ds(lane_start, 4 * CIN)]
                part = jnp.dot(slab.reshape(rows, 4 * CIN), band_ref[tap],
                               preferred_element_type=jnp.float32)
                acc = part if acc is None else acc + part
            conv_ref[2 * pair] = acc[:, :CMID]
            conv_ref[2 * pair + 1] = acc[:, CMID:]
            column = jnp.sum(acc, axis=0, keepdims=True)
            total = column if total is None else total + column
        sum_ref[...] = total[:, :CMID] + total[:, CMID:]

    def tile_step(flag, pos_z):
        @pl.when(flag > 0)
        def _():
            for col in range(size_y // TILE):
                @pl.when(pos_y == col)
                def _():
                    tile_conv(col, pos_z * span)

            count = float(rows * TILE * (CMID // GROUPS))
            lane_in = lax.broadcasted_iota(jnp.int32, (CMID, CMID), 0) // (CMID // GROUPS)
            lane_out = lax.broadcasted_iota(jnp.int32, (CMID, CMID), 1) // (CMID // GROUPS)
            indicator = (lane_in == lane_out).astype(jnp.bfloat16)
            mean = group_sum(sum_ref[...], indicator) / count
            total = jnp.zeros((1, CMID), jnp.float32)
            for depth in range(TILE):
                diff = conv_ref[depth] - mean
                total = total + jnp.sum(diff * diff, axis=0, keepdims=True)
            var = group_sum(total, indicator) / count
            scale = lax.rsqrt(var + EPS) * gamma_ref[...]
            shift = beta_ref[...]

            results = [None] * half
            for pick_b in range(2):
                picked = conv_ref[:, pl.ds(pick_b, rows // 2, stride=2), :]
                normed = [
                    jnp.maximum((picked[depth] - mean) * scale + shift, 0.0)
                    .reshape(half, 2, half, CMID)
                    for depth in range(TILE)
                ]
                for pick_a in range(2):
                    corners = [n[:, pick_a].reshape(half * half, CMID).astype(jnp.bfloat16)
                               for n in normed]
                    lhs = jnp.concatenate([
                        jnp.concatenate([corners[2 * depth], corners[2 * depth + 1]], axis=1)
                        for depth in range(half)
                    ], axis=0)
                    part = jnp.dot(lhs, down_ref[pick_a * 2 + pick_b],
                                   preferred_element_type=jnp.float32)
                    for depth in range(half):
                        piece = part[half * half * depth:half * half * (depth + 1)]
                        results[depth] = piece if results[depth] is None else results[depth] + piece
            bias = bias_ref[...]
            merged = jnp.concatenate([r + bias for r in results], axis=1)
            out_ref[:, :, pos_z * half * COUT:(pos_z + 1) * half * COUT] = merged.reshape(
                half, half, half * COUT).astype(jnp.bfloat16)

        @pl.when(flag == 0)
        def _():
            out_ref[:, :, pos_z * half * COUT:(pos_z + 1) * half * COUT] = jnp.zeros(
                (half, half, half * COUT), out_ref.dtype)

    for pos_z in range(tiles_z):
        tile_step(flags_ref[(pos_x * tiles_y + pos_y) * tiles_z + pos_z], pos_z)


def shards(volume, tissue, w_conv, gamma, beta, w_down, b_down):
    own_index = lax.axis_index("gx")
    size_x, size_y, merged = volume.shape
    size_z = merged // CIN
    tiles_x, tiles_y, tiles_z = size_x // TILE, size_y // TILE, size_z // TILE
    half = TILE // 2
    low_x, high_x, low_y, high_y = halo_pieces(volume)
    down = w_down.reshape(4, 2 * CMID, COUT)
    own_tissue = lax.dynamic_slice_in_dim(tissue, own_index * tiles_x, tiles_x, 0)
    flags = own_tissue.reshape(tiles_x * tiles_y * tiles_z).astype(jnp.int32)

    full = lambda shape: pl.BlockSpec(shape, lambda i, j, f: (0,) * len(shape))
    grid_spec = pltpu.PrefetchScalarGridSpec(
        num_scalar_prefetch=1,
        grid=(tiles_x, tiles_y),
        in_specs=[
            full(volume.shape),
            full(low_x.shape),
            full(high_x.shape),
            full(low_y.shape),
            full(high_y.shape),
            full((27, CIN, CMID)),
            full((1, CMID)),
            full((1, CMID)),
            full((4, 2 * CMID, COUT)),
            full((1, COUT)),
        ],
        out_specs=pl.BlockSpec((half, half, size_z // 2 * COUT), lambda i, j, f: (i, j, 0)),
        scratch_shapes=[
            pltpu.VMEM((size_x + 2, size_y + 2 * TILE, merged + 2 * CIN), jnp.bfloat16),
            pltpu.VMEM((TILE, TILE * TILE, CMID), jnp.float32),
            pltpu.VMEM((9, 4 * CIN, 2 * CMID), jnp.bfloat16),
            pltpu.VMEM((1, CMID), jnp.float32),
        ],
    )
    return pl.pallas_call(
        tile_kernel,
        grid_spec=grid_spec,
        out_shape=jax.ShapeDtypeStruct((size_x // 2, size_y // 2, size_z // 2 * COUT),
                                       jnp.bfloat16),
    )(
        flags,
        volume,
        low_x,
        high_x,
        low_y,
        high_y,
        w_conv.reshape(27, CIN, CMID),
        gamma.reshape(1, CMID),
        beta.reshape(1, CMID),
        down,
        b_down.reshape(1, COUT),
    )


def solution(mesh):
    in_specs = (P("gx", "gy", None), P(None, "gy", None), P(), P(), P(), P(), P())
    out_specs = P("gx", "gy", None)
    return jax.shard_map(shards, mesh=mesh, in_specs=in_specs, out_specs=out_specs, check_vma=False)
```

```python
import jax
import jax.numpy as jnp
from jax import lax
from jax.experimental import pallas as pl
from jax.experimental.pallas import tpu as pltpu
from jax.sharding import PartitionSpec as P

CIN = 64
CMID = 128
COUT = 128
GROUPS = 8
TILE = 16
EPS = 1e-05


def neighbour(block, step_x, step_y):
    count_x, count_y = lax.axis_size("gx"), lax.axis_size("gy")
    pairs = []
    for ix in range(count_x):
        for iy in range(count_y):
            tx, ty = ix + step_x, iy + step_y
            if 0 <= tx < count_x and 0 <= ty < count_y:
                pairs.append((ix * count_y + iy, tx * count_y + ty))
    return lax.ppermute(block, ("gx", "gy"), pairs)


def halo_pieces(block):
    low_x = neighbour(block[-1], 1, 0)
    high_x = neighbour(block[0], -1, 0)
    column_hi = jnp.concatenate([low_x[None, -1], block[:, -1], high_x[None, -1]], axis=0)
    column_lo = jnp.concatenate([low_x[None, 0], block[:, 0], high_x[None, 0]], axis=0)
    low_y = neighbour(column_hi, 0, 1)
    high_y = neighbour(column_lo, 0, -1)
    return low_x, high_x, low_y, high_y


def group_sum(row, indicator):
    row = jnp.broadcast_to(row, (8, row.shape[1]))
    total = jnp.zeros(row.shape, jnp.float32)
    rest = row
    for _ in range(3):
        piece = rest.astype(jnp.bfloat16)
        total = total + jnp.dot(piece, indicator, preferred_element_type=jnp.float32)
        rest = rest - piece.astype(jnp.float32)
    return total[0:1]


def tile_kernel(flags_ref, volume_ref, low_x_ref, high_x_ref, low_y_ref, high_y_ref,
                weight_ref, gamma_ref, beta_ref, down_ref, bias_ref, out_ref,
                grown_ref, conv_ref, band_ref, sum_ref, stage_ref, stage_sems):
    pos_x, pos_y = pl.program_id(0), pl.program_id(1)
    tiles_y = pl.num_programs(1)
    rows = TILE * TILE
    half = TILE // 2
    span = TILE * CIN
    size_x, size_y, merged = volume_ref.shape
    tiles_z = merged // span

    @pl.when((pos_x == 0) & (pos_y == 0))
    def _():
        chunks = stage_sems.shape[0]
        chunk_rows = size_x // chunks
        copies = [
            pltpu.make_async_copy(volume_ref.at[pl.ds(chunk * chunk_rows, chunk_rows)],
                                  stage_ref.at[pl.ds(chunk * chunk_rows, chunk_rows)],
                                  stage_sems.at[chunk])
            for chunk in range(chunks)
        ]
        for copy in copies:
            copy.start()
        edge = jnp.zeros((size_x + 2, grown_ref.shape[1], CIN), grown_ref.dtype)
        grown_ref[:, :, 0:CIN] = edge
        grown_ref[:, :, CIN + merged:2 * CIN + merged] = edge
        band_ref[...] = jnp.zeros(band_ref.shape, band_ref.dtype)
        for tap in range(9):
            for depth in range(3):
                taps = weight_ref[3 * tap + depth]
                band_ref[tap, CIN * depth:CIN * (depth + 1), 0:CMID] = taps
                band_ref[tap, CIN * (depth + 1):CIN * (depth + 2), CMID:2 * CMID] = taps

        def place(row, carry):
            grown_ref[row + 1, TILE:TILE + size_y, CIN:CIN + merged] = stage_ref[row]
            return carry

        for chunk in range(chunks):
            copies[chunk].wait()
            lax.fori_loop(chunk * chunk_rows, (chunk + 1) * chunk_rows, place, 0)
        grown_ref[0, TILE:TILE + size_y, CIN:CIN + merged] = low_x_ref[...]
        grown_ref[size_x + 1, TILE:TILE + size_y, CIN:CIN + merged] = high_x_ref[...]
        for row in range(size_x + 2):
            grown_ref[row, TILE - 1:TILE, CIN:CIN + merged] = low_y_ref[row:row + 1, :]
            grown_ref[row, TILE + size_y:TILE + size_y + 1, CIN:CIN + merged] = (
                high_y_ref[row:row + 1, :])

    def tile_conv(col, start):
        total = None
        for pair in range(half):
            lane_start = start + 2 * CIN * pair
            acc = None
            for tap in range(9):
                shift_x, shift_y = tap // 3, tap % 3
                slab = grown_ref[pl.ds(pos_x * TILE + shift_x, TILE),
                                 pl.ds(col * TILE + shift_y + TILE - 1, TILE),
                                 pl.ds(lane_start, 4 * CIN)]
                part = jnp.dot(slab.reshape(rows, 4 * CIN), band_ref[tap],
                               preferred_element_type=jnp.float32)
                acc = part if acc is None else acc + part
            conv_ref[2 * pair] = acc[:, :CMID]
            conv_ref[2 * pair + 1] = acc[:, CMID:]
            column = jnp.sum(acc, axis=0, keepdims=True)
            total = column if total is None else total + column
        sum_ref[...] = total[:, :CMID] + total[:, CMID:]

    def tile_step(flag, pos_z):
        @pl.when(flag > 0)
        def _():
            for col in range(size_y // TILE):
                @pl.when(pos_y == col)
                def _():
                    tile_conv(col, pos_z * span)

            count = float(rows * TILE * (CMID // GROUPS))
            lane_in = lax.broadcasted_iota(jnp.int32, (CMID, CMID), 0) // (CMID // GROUPS)
            lane_out = lax.broadcasted_iota(jnp.int32, (CMID, CMID), 1) // (CMID // GROUPS)
            indicator = (lane_in == lane_out).astype(jnp.bfloat16)
            mean = group_sum(sum_ref[...], indicator) / count
            total = jnp.zeros((1, CMID), jnp.float32)
            for depth in range(TILE):
                diff = conv_ref[depth] - mean
                total = total + jnp.sum(diff * diff, axis=0, keepdims=True)
            var = group_sum(total, indicator) / count
            scale = lax.rsqrt(var + EPS) * gamma_ref[...]
            shift = beta_ref[...]

            results = [None] * half
            for pick_b in range(2):
                picked = conv_ref[:, pl.ds(pick_b, rows // 2, stride=2), :]
                normed = [
                    jnp.maximum((picked[depth] - mean) * scale + shift, 0.0)
                    .reshape(half, 2, half, CMID)
                    for depth in range(TILE)
                ]
                for pick_a in range(2):
                    corners = [n[:, pick_a].reshape(half * half, CMID).astype(jnp.bfloat16)
                               for n in normed]
                    lhs = jnp.concatenate([
                        jnp.concatenate([corners[2 * depth], corners[2 * depth + 1]], axis=1)
                        for depth in range(half)
                    ], axis=0)
                    part = jnp.dot(lhs, down_ref[pick_a * 2 + pick_b],
                                   preferred_element_type=jnp.float32)
                    for depth in range(half):
                        piece = part[half * half * depth:half * half * (depth + 1)]
                        results[depth] = piece if results[depth] is None else results[depth] + piece
            bias = bias_ref[...]
            merged = jnp.concatenate([r + bias for r in results], axis=1)
            out_ref[:, :, pos_z * half * COUT:(pos_z + 1) * half * COUT] = merged.reshape(
                half, half, half * COUT).astype(jnp.bfloat16)

        @pl.when(flag == 0)
        def _():
            out_ref[:, :, pos_z * half * COUT:(pos_z + 1) * half * COUT] = jnp.zeros(
                (half, half, half * COUT), out_ref.dtype)

    for pos_z in range(tiles_z):
        tile_step(flags_ref[(pos_x * tiles_y + pos_y) * tiles_z + pos_z], pos_z)


def shards(volume, tissue, w_conv, gamma, beta, w_down, b_down):
    own_index = lax.axis_index("gx")
    size_x, size_y, merged = volume.shape
    size_z = merged // CIN
    tiles_x, tiles_y, tiles_z = size_x // TILE, size_y // TILE, size_z // TILE
    half = TILE // 2
    low_x, high_x, low_y, high_y = halo_pieces(volume)
    down = w_down.reshape(4, 2 * CMID, COUT)
    own_tissue = lax.dynamic_slice_in_dim(tissue, own_index * tiles_x, tiles_x, 0)
    flags = own_tissue.reshape(tiles_x * tiles_y * tiles_z).astype(jnp.int32)

    full = lambda shape: pl.BlockSpec(shape, lambda i, j, f: (0,) * len(shape))
    grid_spec = pltpu.PrefetchScalarGridSpec(
        num_scalar_prefetch=1,
        grid=(tiles_x, tiles_y),
        in_specs=[
            pl.BlockSpec(memory_space=pl.ANY),
            full(low_x.shape),
            full(high_x.shape),
            full(low_y.shape),
            full(high_y.shape),
            full((27, CIN, CMID)),
            full((1, CMID)),
            full((1, CMID)),
            full((4, 2 * CMID, COUT)),
            full((1, COUT)),
        ],
        out_specs=pl.BlockSpec((half, half, size_z // 2 * COUT), lambda i, j, f: (i, j, 0)),
        scratch_shapes=[
            pltpu.VMEM((size_x + 2, size_y + 2 * TILE, merged + 2 * CIN), jnp.bfloat16),
            pltpu.VMEM((TILE, TILE * TILE, CMID), jnp.float32),
            pltpu.VMEM((9, 4 * CIN, 2 * CMID), jnp.bfloat16),
            pltpu.VMEM((1, CMID), jnp.float32),
            pltpu.VMEM(volume.shape, jnp.bfloat16),
            pltpu.SemaphoreType.DMA((4,)),
        ],
    )
    return pl.pallas_call(
        tile_kernel,
        grid_spec=grid_spec,
        out_shape=jax.ShapeDtypeStruct((size_x // 2, size_y // 2, size_z // 2 * COUT),
                                       jnp.bfloat16),
    )(
        flags,
        volume,
        low_x,
        high_x,
        low_y,
        high_y,
        w_conv.reshape(27, CIN, CMID),
        gamma.reshape(1, CMID),
        beta.reshape(1, CMID),
        down,
        b_down.reshape(1, COUT),
    )


def solution(mesh):
    in_specs = (P("gx", "gy", None), P(None, "gy", None), P(), P(), P(), P(), P())
    out_specs = P("gx", "gy", None)
    return jax.shard_map(shards, mesh=mesh, in_specs=in_specs, out_specs=out_specs, check_vma=False)
```

```python
import jax
import jax.numpy as jnp
from jax import lax
from jax.experimental import pallas as pl
from jax.experimental.pallas import tpu as pltpu
from jax.sharding import PartitionSpec as P

CIN = 64
CMID = 128
COUT = 128
GROUPS = 8
TILE = 16
EPS = 1e-05


def neighbour(block, step_x, step_y):
    count_x, count_y = lax.axis_size("gx"), lax.axis_size("gy")
    pairs = []
    for ix in range(count_x):
        for iy in range(count_y):
            tx, ty = ix + step_x, iy + step_y
            if 0 <= tx < count_x and 0 <= ty < count_y:
                pairs.append((ix * count_y + iy, tx * count_y + ty))
    return lax.ppermute(block, ("gx", "gy"), pairs)


def halo_pieces(block):
    low_x = neighbour(block[-1], 1, 0)
    high_x = neighbour(block[0], -1, 0)
    column_hi = jnp.concatenate([low_x[None, -1], block[:, -1], high_x[None, -1]], axis=0)
    column_lo = jnp.concatenate([low_x[None, 0], block[:, 0], high_x[None, 0]], axis=0)
    low_y = neighbour(column_hi, 0, 1)
    high_y = neighbour(column_lo, 0, -1)
    return low_x, high_x, low_y, high_y


def group_sum(row):
    width = row.shape[1]
    values = jnp.broadcast_to(row, (8, width))
    lane = lax.broadcasted_iota(jnp.int32, (8, width), 1)
    forward = pltpu.roll(lane, 1, 1) == (lane + width - 1) % width
    step = 1
    while step < CMID // GROUPS:
        ahead = jnp.where(forward, pltpu.roll(values, width - step, 1), pltpu.roll(values, step, 1))
        behind = jnp.where(forward, pltpu.roll(values, step, 1), pltpu.roll(values, width - step, 1))
        values = values + jnp.where(jnp.bitwise_and(lane, step) == 0, ahead, behind)
        step *= 2
    return values[0:1]


def tile_kernel(flags_ref, volume_ref, low_x_ref, high_x_ref, low_y_ref, high_y_ref,
                weight_ref, gamma_ref, beta_ref, down_ref, bias_ref, out_ref,
                grown_ref, conv_ref, band_ref, sum_ref, stage_ref, stage_sems):
    pos_x, pos_y = pl.program_id(0), pl.program_id(1)
    tiles_y = pl.num_programs(1)
    rows = TILE * TILE
    half = TILE // 2
    span = TILE * CIN
    size_x, size_y, merged = volume_ref.shape
    tiles_z = merged // span

    @pl.when((pos_x == 0) & (pos_y == 0))
    def _():
        chunks = stage_sems.shape[0]
        chunk_rows = size_x // chunks
        copies = [
            pltpu.make_async_copy(volume_ref.at[pl.ds(chunk * chunk_rows, chunk_rows)],
                                  stage_ref.at[pl.ds(chunk * chunk_rows, chunk_rows)],
                                  stage_sems.at[chunk])
            for chunk in range(chunks)
        ]
        for copy in copies:
            copy.start()
        edge = jnp.zeros((size_x + 2, grown_ref.shape[1], CIN), grown_ref.dtype)
        grown_ref[:, :, 0:CIN] = edge
        grown_ref[:, :, CIN + merged:2 * CIN + merged] = edge
        band_ref[...] = jnp.zeros(band_ref.shape, band_ref.dtype)
        for tap in range(9):
            for depth in range(3):
                taps = weight_ref[3 * tap + depth]
                band_ref[tap, CIN * depth:CIN * (depth + 1), 0:CMID] = taps
                band_ref[tap, CIN * (depth + 1):CIN * (depth + 2), CMID:2 * CMID] = taps

        def place(row, carry):
            grown_ref[row + 1, TILE:TILE + size_y, CIN:CIN + merged] = stage_ref[row]
            return carry

        for chunk in range(chunks):
            copies[chunk].wait()
            lax.fori_loop(chunk * chunk_rows, (chunk + 1) * chunk_rows, place, 0)
        grown_ref[0, TILE:TILE + size_y, CIN:CIN + merged] = low_x_ref[...]
        grown_ref[size_x + 1, TILE:TILE + size_y, CIN:CIN + merged] = high_x_ref[...]
        for row in range(size_x + 2):
            grown_ref[row, TILE - 1:TILE, CIN:CIN + merged] = low_y_ref[row:row + 1, :]
            grown_ref[row, TILE + size_y:TILE + size_y + 1, CIN:CIN + merged] = (
                high_y_ref[row:row + 1, :])

    def tile_conv(col, start):
        total = None
        for pair in range(half):
            lane_start = start + 2 * CIN * pair
            acc = None
            for tap in range(9):
                shift_x, shift_y = tap // 3, tap % 3
                slab = grown_ref[pl.ds(pos_x * TILE + shift_x, TILE),
                                 pl.ds(col * TILE + shift_y + TILE - 1, TILE),
                                 pl.ds(lane_start, 4 * CIN)]
                part = jnp.dot(slab.reshape(rows, 4 * CIN), band_ref[tap],
                               preferred_element_type=jnp.float32)
                acc = part if acc is None else acc + part
            conv_ref[2 * pair] = acc[:, :CMID]
            conv_ref[2 * pair + 1] = acc[:, CMID:]
            column = jnp.sum(acc, axis=0, keepdims=True)
            total = column if total is None else total + column
        sum_ref[...] = total[:, :CMID] + total[:, CMID:]

    def tile_step(flag, pos_z):
        @pl.when(flag > 0)
        def _():
            for col in range(size_y // TILE):
                @pl.when(pos_y == col)
                def _():
                    tile_conv(col, pos_z * span)

            count = float(rows * TILE * (CMID // GROUPS))
            mean = group_sum(sum_ref[...]) / count
            total = jnp.zeros((1, CMID), jnp.float32)
            for depth in range(TILE):
                diff = conv_ref[depth] - mean
                total = total + jnp.sum(diff * diff, axis=0, keepdims=True)
            var = group_sum(total) / count
            scale = lax.rsqrt(var + EPS) * gamma_ref[...]
            shift = beta_ref[...]

            results = [None] * half
            for pick_b in range(2):
                picked = conv_ref[:, pl.ds(pick_b, rows // 2, stride=2), :]
                normed = [
                    jnp.maximum((picked[depth] - mean) * scale + shift, 0.0)
                    .reshape(half, 2, half, CMID)
                    for depth in range(TILE)
                ]
                for pick_a in range(2):
                    corners = [n[:, pick_a].reshape(half * half, CMID).astype(jnp.bfloat16)
                               for n in normed]
                    lhs = jnp.concatenate([
                        jnp.concatenate([corners[2 * depth], corners[2 * depth + 1]], axis=1)
                        for depth in range(half)
                    ], axis=0)
                    part = jnp.dot(lhs, down_ref[pick_a * 2 + pick_b],
                                   preferred_element_type=jnp.float32)
                    for depth in range(half):
                        piece = part[half * half * depth:half * half * (depth + 1)]
                        results[depth] = piece if results[depth] is None else results[depth] + piece
            bias = bias_ref[...]
            merged = jnp.concatenate([r + bias for r in results], axis=1)
            out_ref[:, :, pos_z * half * COUT:(pos_z + 1) * half * COUT] = merged.reshape(
                half, half, half * COUT).astype(jnp.bfloat16)

        @pl.when(flag == 0)
        def _():
            out_ref[:, :, pos_z * half * COUT:(pos_z + 1) * half * COUT] = jnp.zeros(
                (half, half, half * COUT), out_ref.dtype)

    for pos_z in range(tiles_z):
        tile_step(flags_ref[(pos_x * tiles_y + pos_y) * tiles_z + pos_z], pos_z)


def shards(volume, tissue, w_conv, gamma, beta, w_down, b_down):
    own_index = lax.axis_index("gx")
    size_x, size_y, merged = volume.shape
    size_z = merged // CIN
    tiles_x, tiles_y, tiles_z = size_x // TILE, size_y // TILE, size_z // TILE
    half = TILE // 2
    low_x, high_x, low_y, high_y = halo_pieces(volume)
    down = w_down.reshape(4, 2 * CMID, COUT)
    own_tissue = lax.dynamic_slice_in_dim(tissue, own_index * tiles_x, tiles_x, 0)
    flags = own_tissue.reshape(tiles_x * tiles_y * tiles_z).astype(jnp.int32)

    full = lambda shape: pl.BlockSpec(shape, lambda i, j, f: (0,) * len(shape))
    grid_spec = pltpu.PrefetchScalarGridSpec(
        num_scalar_prefetch=1,
        grid=(tiles_x, tiles_y),
        in_specs=[
            pl.BlockSpec(memory_space=pl.ANY),
            full(low_x.shape),
            full(high_x.shape),
            full(low_y.shape),
            full(high_y.shape),
            full((27, CIN, CMID)),
            full((1, CMID)),
            full((1, CMID)),
            full((4, 2 * CMID, COUT)),
            full((1, COUT)),
        ],
        out_specs=pl.BlockSpec((half, half, size_z // 2 * COUT), lambda i, j, f: (i, j, 0)),
        scratch_shapes=[
            pltpu.VMEM((size_x + 2, size_y + 2 * TILE, merged + 2 * CIN), jnp.bfloat16),
            pltpu.VMEM((TILE, TILE * TILE, CMID), jnp.float32),
            pltpu.VMEM((9, 4 * CIN, 2 * CMID), jnp.bfloat16),
            pltpu.VMEM((1, CMID), jnp.float32),
            pltpu.VMEM(volume.shape, jnp.bfloat16),
            pltpu.SemaphoreType.DMA((4,)),
        ],
    )
    return pl.pallas_call(
        tile_kernel,
        grid_spec=grid_spec,
        out_shape=jax.ShapeDtypeStruct((size_x // 2, size_y // 2, size_z // 2 * COUT),
                                       jnp.bfloat16),
    )(
        flags,
        volume,
        low_x,
        high_x,
        low_y,
        high_y,
        w_conv.reshape(27, CIN, CMID),
        gamma.reshape(1, CMID),
        beta.reshape(1, CMID),
        down,
        b_down.reshape(1, COUT),
    )


def solution(mesh):
    in_specs = (P("gx", "gy", None), P(None, "gy", None), P(), P(), P(), P(), P())
    out_specs = P("gx", "gy", None)
    return jax.shard_map(shards, mesh=mesh, in_specs=in_specs, out_specs=out_specs, check_vma=False)
```

```python
import jax
import jax.numpy as jnp
from jax import lax
from jax.experimental import pallas as pl
from jax.experimental.pallas import tpu as pltpu
from jax.sharding import PartitionSpec as P

CIN = 64
CMID = 128
COUT = 128
GROUPS = 8
TILE = 16
EPS = 1e-05


def neighbour(block, step_x, step_y):
    count_x, count_y = lax.axis_size("gx"), lax.axis_size("gy")
    pairs = []
    for ix in range(count_x):
        for iy in range(count_y):
            tx, ty = ix + step_x, iy + step_y
            if 0 <= tx < count_x and 0 <= ty < count_y:
                pairs.append((ix * count_y + iy, tx * count_y + ty))
    return lax.ppermute(block, ("gx", "gy"), pairs)


def halo_pieces(block):
    low_x = neighbour(block[-1], 1, 0)
    high_x = neighbour(block[0], -1, 0)
    column_hi = jnp.concatenate([low_x[None, -1], block[:, -1], high_x[None, -1]], axis=0)
    column_lo = jnp.concatenate([low_x[None, 0], block[:, 0], high_x[None, 0]], axis=0)
    low_y = neighbour(column_hi, 0, 1)
    high_y = neighbour(column_lo, 0, -1)
    return low_x, high_x, low_y, high_y


def group_sum(row, indicator):
    row = jnp.broadcast_to(row, (8, row.shape[1]))
    total = jnp.zeros(row.shape, jnp.float32)
    rest = row
    for _ in range(3):
        piece = rest.astype(jnp.bfloat16)
        total = total + jnp.dot(piece, indicator, preferred_element_type=jnp.float32)
        rest = rest - piece.astype(jnp.float32)
    return total[0:1]


def tile_kernel(flags_ref, volume_ref, low_x_ref, high_x_ref, low_y_ref, high_y_ref,
                weight_ref, gamma_ref, beta_ref, down_ref, bias_ref, out_ref,
                grown_ref, conv_ref, band_ref, sum_ref, stage_ref, stage_sems):
    pos_x, pos_y = pl.program_id(0), pl.program_id(1)
    tiles_y = pl.num_programs(1)
    rows = TILE * TILE
    half = TILE // 2
    span = TILE * CIN
    size_x, size_y, merged = volume_ref.shape
    tiles_z = merged // span

    @pl.when((pos_x == 0) & (pos_y == 0))
    def _():
        chunks = stage_sems.shape[0]
        chunk_rows = size_x // chunks
        copies = [
            pltpu.make_async_copy(volume_ref.at[pl.ds(chunk * chunk_rows, chunk_rows)],
                                  stage_ref.at[pl.ds(chunk * chunk_rows, chunk_rows)],
                                  stage_sems.at[chunk])
            for chunk in range(chunks)
        ]
        for copy in copies:
            copy.start()
        edge = jnp.zeros((size_x + 2, grown_ref.shape[1], CIN), grown_ref.dtype)
        grown_ref[:, :, 0:CIN] = edge
        grown_ref[:, :, CIN + merged:2 * CIN + merged] = edge
        empty = jnp.zeros((CIN, CMID), band_ref.dtype)
        for tap in range(9):
            band_ref[tap, 3 * CIN:4 * CIN, 0:CMID] = empty
            band_ref[tap, 0:CIN, CMID:2 * CMID] = empty
            for depth in range(3):
                taps = weight_ref[3 * tap + depth]
                band_ref[tap, CIN * depth:CIN * (depth + 1), 0:CMID] = taps
                band_ref[tap, CIN * (depth + 1):CIN * (depth + 2), CMID:2 * CMID] = taps

        def place(row, carry):
            grown_ref[row + 1, TILE:TILE + size_y, CIN:CIN + merged] = stage_ref[row]
            return carry

        for chunk in range(chunks):
            copies[chunk].wait()
            lax.fori_loop(chunk * chunk_rows, (chunk + 1) * chunk_rows, place, 0)
        grown_ref[0, TILE:TILE + size_y, CIN:CIN + merged] = low_x_ref[...]
        grown_ref[size_x + 1, TILE:TILE + size_y, CIN:CIN + merged] = high_x_ref[...]
        for row in range(size_x + 2):
            grown_ref[row, TILE - 1:TILE, CIN:CIN + merged] = low_y_ref[row:row + 1, :]
            grown_ref[row, TILE + size_y:TILE + size_y + 1, CIN:CIN + merged] = (
                high_y_ref[row:row + 1, :])

    def tile_conv(col, start):
        total = None
        for pair in range(half):
            lane_start = start + 2 * CIN * pair
            acc = None
            for tap in range(9):
                shift_x, shift_y = tap // 3, tap % 3
                slab = grown_ref[pl.ds(pos_x * TILE + shift_x, TILE),
                                 pl.ds(col * TILE + shift_y + TILE - 1, TILE),
                                 pl.ds(lane_start, 4 * CIN)]
                part = jnp.dot(slab.reshape(rows, 4 * CIN), band_ref[tap],
                               preferred_element_type=jnp.float32)
                acc = part if acc is None else acc + part
            conv_ref[2 * pair] = acc[:, :CMID]
            conv_ref[2 * pair + 1] = acc[:, CMID:]
            column = jnp.sum(acc, axis=0, keepdims=True)
            total = column if total is None else total + column
        sum_ref[...] = total[:, :CMID] + total[:, CMID:]

    def tile_step(flag, pos_z):
        @pl.when(flag > 0)
        def _():
            for col in range(size_y // TILE):
                @pl.when(pos_y == col)
                def _():
                    tile_conv(col, pos_z * span)

            count = float(rows * TILE * (CMID // GROUPS))
            lane_in = lax.broadcasted_iota(jnp.int32, (CMID, CMID), 0) // (CMID // GROUPS)
            lane_out = lax.broadcasted_iota(jnp.int32, (CMID, CMID), 1) // (CMID // GROUPS)
            indicator = (lane_in == lane_out).astype(jnp.bfloat16)
            mean = group_sum(sum_ref[...], indicator) / count
            total = jnp.zeros((1, CMID), jnp.float32)
            for depth in range(TILE):
                diff = conv_ref[depth] - mean
                total = total + jnp.sum(diff * diff, axis=0, keepdims=True)
            var = group_sum(total, indicator) / count
            scale = lax.rsqrt(var + EPS) * gamma_ref[...]
            shift = beta_ref[...]

            results = [None] * half
            for pick_b in range(2):
                picked = conv_ref[:, pl.ds(pick_b, rows // 2, stride=2), :]
                normed = [
                    jnp.maximum((picked[depth] - mean) * scale + shift, 0.0)
                    .reshape(half, 2, half, CMID)
                    for depth in range(TILE)
                ]
                for pick_a in range(2):
                    corners = [n[:, pick_a].reshape(half * half, CMID).astype(jnp.bfloat16)
                               for n in normed]
                    lhs = jnp.concatenate([
                        jnp.concatenate([corners[2 * depth], corners[2 * depth + 1]], axis=1)
                        for depth in range(half)
                    ], axis=0)
                    part = jnp.dot(lhs, down_ref[pick_a * 2 + pick_b],
                                   preferred_element_type=jnp.float32)
                    for depth in range(half):
                        piece = part[half * half * depth:half * half * (depth + 1)]
                        results[depth] = piece if results[depth] is None else results[depth] + piece
            bias = bias_ref[...]
            merged = jnp.concatenate([r + bias for r in results], axis=1)
            out_ref[:, :, pos_z * half * COUT:(pos_z + 1) * half * COUT] = merged.reshape(
                half, half, half * COUT).astype(jnp.bfloat16)

        @pl.when(flag == 0)
        def _():
            out_ref[:, :, pos_z * half * COUT:(pos_z + 1) * half * COUT] = jnp.zeros(
                (half, half, half * COUT), out_ref.dtype)

    for pos_z in range(tiles_z):
        tile_step(flags_ref[(pos_x * tiles_y + pos_y) * tiles_z + pos_z], pos_z)


def shards(volume, tissue, w_conv, gamma, beta, w_down, b_down):
    own_index = lax.axis_index("gx")
    size_x, size_y, merged = volume.shape
    size_z = merged // CIN
    tiles_x, tiles_y, tiles_z = size_x // TILE, size_y // TILE, size_z // TILE
    half = TILE // 2
    low_x, high_x, low_y, high_y = halo_pieces(volume)
    down = w_down.reshape(4, 2 * CMID, COUT)
    own_tissue = lax.dynamic_slice_in_dim(tissue, own_index * tiles_x, tiles_x, 0)
    flags = own_tissue.reshape(tiles_x * tiles_y * tiles_z).astype(jnp.int32)

    full = lambda shape: pl.BlockSpec(shape, lambda i, j, f: (0,) * len(shape))
    grid_spec = pltpu.PrefetchScalarGridSpec(
        num_scalar_prefetch=1,
        grid=(tiles_x, tiles_y),
        in_specs=[
            pl.BlockSpec(memory_space=pl.ANY),
            full(low_x.shape),
            full(high_x.shape),
            full(low_y.shape),
            full(high_y.shape),
            full((27, CIN, CMID)),
            full((1, CMID)),
            full((1, CMID)),
            full((4, 2 * CMID, COUT)),
            full((1, COUT)),
        ],
        out_specs=pl.BlockSpec((half, half, size_z // 2 * COUT), lambda i, j, f: (i, j, 0)),
        scratch_shapes=[
            pltpu.VMEM((size_x + 2, size_y + 2 * TILE, merged + 2 * CIN), jnp.bfloat16),
            pltpu.VMEM((TILE, TILE * TILE, CMID), jnp.float32),
            pltpu.VMEM((9, 4 * CIN, 2 * CMID), jnp.bfloat16),
            pltpu.VMEM((1, CMID), jnp.float32),
            pltpu.VMEM(volume.shape, jnp.bfloat16),
            pltpu.SemaphoreType.DMA((4,)),
        ],
    )
    return pl.pallas_call(
        tile_kernel,
        grid_spec=grid_spec,
        out_shape=jax.ShapeDtypeStruct((size_x // 2, size_y // 2, size_z // 2 * COUT),
                                       jnp.bfloat16),
    )(
        flags,
        volume,
        low_x,
        high_x,
        low_y,
        high_y,
        w_conv.reshape(27, CIN, CMID),
        gamma.reshape(1, CMID),
        beta.reshape(1, CMID),
        down,
        b_down.reshape(1, COUT),
    )


def solution(mesh):
    in_specs = (P("gx", "gy", None), P(None, "gy", None), P(), P(), P(), P(), P())
    out_specs = P("gx", "gy", None)
    return jax.shard_map(shards, mesh=mesh, in_specs=in_specs, out_specs=out_specs, check_vma=False)
```

```python
import jax
import jax.numpy as jnp
from jax import lax
from jax.experimental import pallas as pl
from jax.experimental.pallas import tpu as pltpu
from jax.sharding import PartitionSpec as P

CIN = 64
CMID = 128
COUT = 128
GROUPS = 8
TILE = 16
EPS = 1e-05


def neighbour(block, step_x, step_y):
    count_x, count_y = lax.axis_size("gx"), lax.axis_size("gy")
    pairs = []
    for ix in range(count_x):
        for iy in range(count_y):
            tx, ty = ix + step_x, iy + step_y
            if 0 <= tx < count_x and 0 <= ty < count_y:
                pairs.append((ix * count_y + iy, tx * count_y + ty))
    return lax.ppermute(block, ("gx", "gy"), pairs)


def halo_pieces(block):
    low_x = neighbour(block[-1], 1, 0)
    high_x = neighbour(block[0], -1, 0)
    column_hi = jnp.concatenate([low_x[None, -1], block[:, -1], high_x[None, -1]], axis=0)
    column_lo = jnp.concatenate([low_x[None, 0], block[:, 0], high_x[None, 0]], axis=0)
    low_y = neighbour(column_hi, 0, 1)
    high_y = neighbour(column_lo, 0, -1)
    return low_x, high_x, low_y, high_y


def group_sum(row, indicator):
    row = jnp.broadcast_to(row, (8, row.shape[1]))
    total = jnp.zeros(row.shape, jnp.float32)
    rest = row
    for _ in range(3):
        piece = rest.astype(jnp.bfloat16)
        total = total + jnp.dot(piece, indicator, preferred_element_type=jnp.float32)
        rest = rest - piece.astype(jnp.float32)
    return total[0:1]


def tile_kernel(flags_ref, volume_ref, low_x_ref, high_x_ref, low_y_ref, high_y_ref,
                weight_ref, gamma_ref, beta_ref, down_ref, bias_ref, out_ref,
                grown_ref, conv_ref, band_ref, sum_ref, stage_ref, stage_sems):
    pos_x, pos_y = pl.program_id(0), pl.program_id(1)
    tiles_y = pl.num_programs(1)
    rows = TILE * TILE
    half = TILE // 2
    span = TILE * CIN
    size_x, size_y, merged = volume_ref.shape
    tiles_z = merged // span

    @pl.when((pos_x == 0) & (pos_y == 0))
    def _():
        chunks = stage_sems.shape[0]
        chunk_rows = size_x // chunks
        copies = [
            pltpu.make_async_copy(volume_ref.at[pl.ds(chunk * chunk_rows, chunk_rows)],
                                  stage_ref.at[pl.ds(chunk * chunk_rows, chunk_rows)],
                                  stage_sems.at[chunk])
            for chunk in range(chunks)
        ]
        for copy in copies:
            copy.start()
        edge = jnp.zeros((size_x + 2, grown_ref.shape[1], CIN), grown_ref.dtype)
        grown_ref[:, :, 0:CIN] = edge
        grown_ref[:, :, CIN + merged:2 * CIN + merged] = edge
        band_ref[...] = jnp.zeros(band_ref.shape, band_ref.dtype)
        for tap in range(9):
            for depth in range(3):
                taps = weight_ref[3 * tap + depth]
                band_ref[tap, CIN * depth:CIN * (depth + 1), 0:CMID] = taps
                band_ref[tap, CIN * (depth + 1):CIN * (depth + 2), CMID:2 * CMID] = taps

        def place(row, carry):
            grown_ref[row + 1, TILE:TILE + size_y, CIN:CIN + merged] = stage_ref[row]
            return carry

        for chunk in range(chunks):
            copies[chunk].wait()
            lax.fori_loop(chunk * chunk_rows, (chunk + 1) * chunk_rows, place, 0)
        grown_ref[0, TILE:TILE + size_y, CIN:CIN + merged] = low_x_ref[...]
        grown_ref[size_x + 1, TILE:TILE + size_y, CIN:CIN + merged] = high_x_ref[...]
        for row in range(size_x + 2):
            grown_ref[row, TILE - 1:TILE, CIN:CIN + merged] = low_y_ref[row:row + 1, :]
            grown_ref[row, TILE + size_y:TILE + size_y + 1, CIN:CIN + merged] = (
                high_y_ref[row:row + 1, :])

    def tile_conv(col, start):
        total = None
        for pair in range(half):
            lane_start = start + 2 * CIN * pair
            acc = None
            for tap in range(9):
                shift_x, shift_y = tap // 3, tap % 3
                slab = grown_ref[pl.ds(pos_x * TILE + shift_x, TILE),
                                 pl.ds(col * TILE + shift_y + TILE - 1, TILE),
                                 pl.ds(lane_start, 4 * CIN)]
                part = jnp.dot(slab.reshape(rows, 4 * CIN), band_ref[tap],
                               preferred_element_type=jnp.float32)
                acc = part if acc is None else acc + part
            conv_ref[2 * pair] = acc[:, :CMID]
            conv_ref[2 * pair + 1] = acc[:, CMID:]
            column = jnp.sum(acc, axis=0, keepdims=True)
            total = column if total is None else total + column
        sum_ref[...] = total[:, :CMID] + total[:, CMID:]

    def tile_step(flag, pos_z):
        @pl.when(flag > 0)
        def _():
            for col in range(size_y // TILE):
                @pl.when(pos_y == col)
                def _():
                    tile_conv(col, pos_z * span)

            count = float(rows * TILE * (CMID // GROUPS))
            lane_in = lax.broadcasted_iota(jnp.int32, (CMID, CMID), 0) // (CMID // GROUPS)
            lane_out = lax.broadcasted_iota(jnp.int32, (CMID, CMID), 1) // (CMID // GROUPS)
            indicator = (lane_in == lane_out).astype(jnp.bfloat16)
            mean = group_sum(sum_ref[...], indicator) / count
            total = jnp.zeros((1, CMID), jnp.float32)
            for depth in range(TILE):
                diff = conv_ref[depth] - mean
                total = total + jnp.sum(diff * diff, axis=0, keepdims=True)
            var = group_sum(total, indicator) / count
            scale = lax.rsqrt(var + EPS) * gamma_ref[...]
            shift = beta_ref[...]

            results = [None] * half
            for pick_b in range(2):
                picked = conv_ref[:, pl.ds(pick_b, rows // 2, stride=2), :]
                normed = [
                    jnp.maximum((picked[depth] - mean) * scale + shift, 0.0)
                    .reshape(half, 2, half, CMID)
                    for depth in range(TILE)
                ]
                for pick_a in range(2):
                    corners = [n[:, pick_a].reshape(half * half, CMID).astype(jnp.bfloat16)
                               for n in normed]
                    lhs = jnp.concatenate([
                        jnp.concatenate([corners[2 * depth], corners[2 * depth + 1]], axis=1)
                        for depth in range(half)
                    ], axis=0)
                    part = jnp.dot(lhs, down_ref[pick_a * 2 + pick_b],
                                   preferred_element_type=jnp.float32)
                    for depth in range(half):
                        piece = part[half * half * depth:half * half * (depth + 1)]
                        results[depth] = piece if results[depth] is None else results[depth] + piece
            bias = bias_ref[...]
            merged = jnp.concatenate([r + bias for r in results], axis=1)
            out_ref[:, :, pos_z * half * COUT:(pos_z + 1) * half * COUT] = merged.reshape(
                half, half, half * COUT).astype(jnp.bfloat16)

        @pl.when(flag == 0)
        def _():
            out_ref[:, :, pos_z * half * COUT:(pos_z + 1) * half * COUT] = jnp.zeros(
                (half, half, half * COUT), out_ref.dtype)

    for pos_z in range(tiles_z):
        tile_step(flags_ref[(pos_x * tiles_y + pos_y) * tiles_z + pos_z], pos_z)


def shards(volume, tissue, w_conv, gamma, beta, w_down, b_down):
    own_index = lax.axis_index("gx")
    size_x, size_y, merged = volume.shape
    size_z = merged // CIN
    tiles_x, tiles_y, tiles_z = size_x // TILE, size_y // TILE, size_z // TILE
    half = TILE // 2
    low_x, high_x, low_y, high_y = halo_pieces(volume)
    down = w_down.reshape(4, 2 * CMID, COUT)
    own_tissue = lax.dynamic_slice_in_dim(tissue, own_index * tiles_x, tiles_x, 0)
    flags = own_tissue.reshape(tiles_x * tiles_y * tiles_z).astype(jnp.int32)

    full = lambda shape: pl.BlockSpec(shape, lambda i, j, f: (0,) * len(shape))
    grid_spec = pltpu.PrefetchScalarGridSpec(
        num_scalar_prefetch=1,
        grid=(tiles_x, tiles_y),
        in_specs=[
            pl.BlockSpec(memory_space=pl.ANY),
            full(low_x.shape),
            full(high_x.shape),
            full(low_y.shape),
            full(high_y.shape),
            full((27, CIN, CMID)),
            full((1, CMID)),
            full((1, CMID)),
            full((4, 2 * CMID, COUT)),
            full((1, COUT)),
        ],
        out_specs=pl.BlockSpec((half, half, size_z // 2 * COUT), lambda i, j, f: (i, j, 0)),
        scratch_shapes=[
            pltpu.VMEM((size_x + 2, size_y + 2 * TILE, merged + 2 * CIN), jnp.bfloat16),
            pltpu.VMEM((TILE, TILE * TILE, CMID), jnp.float32),
            pltpu.VMEM((9, 4 * CIN, 2 * CMID), jnp.bfloat16),
            pltpu.VMEM((1, CMID), jnp.float32),
            pltpu.VMEM(volume.shape, jnp.bfloat16),
            pltpu.SemaphoreType.DMA((8,)),
        ],
    )
    return pl.pallas_call(
        tile_kernel,
        grid_spec=grid_spec,
        out_shape=jax.ShapeDtypeStruct((size_x // 2, size_y // 2, size_z // 2 * COUT),
                                       jnp.bfloat16),
    )(
        flags,
        volume,
        low_x,
        high_x,
        low_y,
        high_y,
        w_conv.reshape(27, CIN, CMID),
        gamma.reshape(1, CMID),
        beta.reshape(1, CMID),
        down,
        b_down.reshape(1, COUT),
    )


def solution(mesh):
    in_specs = (P("gx", "gy", None), P(None, "gy", None), P(), P(), P(), P(), P())
    out_specs = P("gx", "gy", None)
    return jax.shard_map(shards, mesh=mesh, in_specs=in_specs, out_specs=out_specs, check_vma=False)
```

```python
import jax
import jax.numpy as jnp
from jax import lax
from jax.experimental import pallas as pl
from jax.experimental.pallas import tpu as pltpu
from jax.sharding import PartitionSpec as P

CIN = 64
CMID = 128
COUT = 128
GROUPS = 8
TILE = 16
EPS = 1e-05


def neighbour(block, step_x, step_y):
    count_x, count_y = lax.axis_size("gx"), lax.axis_size("gy")
    pairs = []
    for ix in range(count_x):
        for iy in range(count_y):
            tx, ty = ix + step_x, iy + step_y
            if 0 <= tx < count_x and 0 <= ty < count_y:
                pairs.append((ix * count_y + iy, tx * count_y + ty))
    return lax.ppermute(block, ("gx", "gy"), pairs)


def halo_pieces(block):
    low_x = neighbour(block[-1], 1, 0)
    high_x = neighbour(block[0], -1, 0)
    column_hi = jnp.concatenate([low_x[None, -1], block[:, -1], high_x[None, -1]], axis=0)
    column_lo = jnp.concatenate([low_x[None, 0], block[:, 0], high_x[None, 0]], axis=0)
    low_y = neighbour(column_hi, 0, 1)
    high_y = neighbour(column_lo, 0, -1)
    return low_x, high_x, low_y, high_y


def group_sum(row, indicator):
    row = jnp.broadcast_to(row, (8, row.shape[1]))
    total = jnp.zeros(row.shape, jnp.float32)
    rest = row
    for _ in range(3):
        piece = rest.astype(jnp.bfloat16)
        total = total + jnp.dot(piece, indicator, preferred_element_type=jnp.float32)
        rest = rest - piece.astype(jnp.float32)
    return total[0:1]


def tile_kernel(flags_ref, volume_ref, low_x_ref, high_x_ref, low_y_ref, high_y_ref,
                weight_ref, gamma_ref, beta_ref, down_ref, bias_ref, out_ref,
                grown_ref, conv_ref, band_ref, sum_ref, stage_ref, stage_sems):
    pos_x, pos_y = pl.program_id(0), pl.program_id(1)
    tiles_y = pl.num_programs(1)
    rows = TILE * TILE
    half = TILE // 2
    span = TILE * CIN
    size_x, size_y, merged = volume_ref.shape
    tiles_z = merged // span

    @pl.when((pos_x == 0) & (pos_y == 0))
    def _():
        chunks = stage_sems.shape[0]
        chunk_rows = size_x // chunks
        copies = [
            pltpu.make_async_copy(volume_ref.at[pl.ds(chunk * chunk_rows, chunk_rows)],
                                  stage_ref.at[pl.ds(chunk * chunk_rows, chunk_rows)],
                                  stage_sems.at[chunk])
            for chunk in range(chunks)
        ]
        for copy in copies:
            copy.start()
        edge = jnp.zeros((size_x + 2, grown_ref.shape[1], CIN), grown_ref.dtype)
        grown_ref[:, :, 0:CIN] = edge
        grown_ref[:, :, CIN + merged:2 * CIN + merged] = edge
        band_ref[...] = jnp.zeros(band_ref.shape, band_ref.dtype)
        for tap in range(9):
            for depth in range(3):
                taps = weight_ref[3 * tap + depth]
                band_ref[tap, CIN * depth:CIN * (depth + 1), 0:CMID] = taps
                band_ref[tap, CIN * (depth + 1):CIN * (depth + 2), CMID:2 * CMID] = taps

        def place(row, carry):
            grown_ref[row + 1, TILE:TILE + size_y, CIN:CIN + merged] = stage_ref[row]
            return carry

        for chunk in range(chunks):
            copies[chunk].wait()
            lax.fori_loop(chunk * chunk_rows, (chunk + 1) * chunk_rows, place, 0)
        grown_ref[0, TILE:TILE + size_y, CIN:CIN + merged] = low_x_ref[...]
        grown_ref[size_x + 1, TILE:TILE + size_y, CIN:CIN + merged] = high_x_ref[...]
        for row in range(size_x + 2):
            grown_ref[row, TILE - 1:TILE, CIN:CIN + merged] = low_y_ref[row:row + 1, :]
            grown_ref[row, TILE + size_y:TILE + size_y + 1, CIN:CIN + merged] = (
                high_y_ref[row:row + 1, :])

    def tile_conv(col, start):
        total = None
        for pair in range(half):
            lane_start = start + 2 * CIN * pair
            acc = None
            for tap in range(9):
                shift_x, shift_y = tap // 3, tap % 3
                slab = grown_ref[pl.ds(pos_x * TILE + shift_x, TILE),
                                 pl.ds(col * TILE + shift_y + TILE - 1, TILE),
                                 pl.ds(lane_start, 4 * CIN)]
                part = jnp.dot(slab.reshape(rows, 4 * CIN), band_ref[tap],
                               preferred_element_type=jnp.float32)
                acc = part if acc is None else acc + part
            conv_ref[2 * pair] = acc[:, :CMID]
            conv_ref[2 * pair + 1] = acc[:, CMID:]
            column = jnp.sum(acc, axis=0, keepdims=True)
            total = column if total is None else total + column
        sum_ref[...] = total[:, :CMID] + total[:, CMID:]

    def tile_step(flag, pos_z):
        @pl.when(flag > 0)
        def _():
            for col in range(size_y // TILE):
                @pl.when(pos_y == col)
                def _():
                    tile_conv(col, pos_z * span)

            count = float(rows * TILE * (CMID // GROUPS))
            mean = group_sum(sum_ref[...], indicator) / count
            total = jnp.zeros((1, CMID), jnp.float32)
            for depth in range(TILE):
                diff = conv_ref[depth] - mean
                total = total + jnp.sum(diff * diff, axis=0, keepdims=True)
            var = group_sum(total, indicator) / count
            scale = lax.rsqrt(var + EPS) * gamma_ref[...]
            shift = beta_ref[...]

            results = [None] * half
            for pick_b in range(2):
                picked = conv_ref[:, pl.ds(pick_b, rows // 2, stride=2), :]
                normed = [
                    jnp.maximum((picked[depth] - mean) * scale + shift, 0.0)
                    .reshape(half, 2, half, CMID)
                    for depth in range(TILE)
                ]
                for pick_a in range(2):
                    corners = [n[:, pick_a].reshape(half * half, CMID).astype(jnp.bfloat16)
                               for n in normed]
                    lhs = jnp.concatenate([
                        jnp.concatenate([corners[2 * depth], corners[2 * depth + 1]], axis=1)
                        for depth in range(half)
                    ], axis=0)
                    part = jnp.dot(lhs, down_ref[pick_a * 2 + pick_b],
                                   preferred_element_type=jnp.float32)
                    for depth in range(half):
                        piece = part[half * half * depth:half * half * (depth + 1)]
                        results[depth] = piece if results[depth] is None else results[depth] + piece
            bias = bias_ref[...]
            merged = jnp.concatenate([r + bias for r in results], axis=1)
            out_ref[:, :, pos_z * half * COUT:(pos_z + 1) * half * COUT] = merged.reshape(
                half, half, half * COUT).astype(jnp.bfloat16)

        @pl.when(flag == 0)
        def _():
            out_ref[:, :, pos_z * half * COUT:(pos_z + 1) * half * COUT] = jnp.zeros(
                (half, half, half * COUT), out_ref.dtype)

    lane_in = lax.broadcasted_iota(jnp.int32, (CMID, CMID), 0) // (CMID // GROUPS)
    lane_out = lax.broadcasted_iota(jnp.int32, (CMID, CMID), 1) // (CMID // GROUPS)
    indicator = (lane_in == lane_out).astype(jnp.bfloat16)
    for pos_z in range(tiles_z):
        tile_step(flags_ref[(pos_x * tiles_y + pos_y) * tiles_z + pos_z], pos_z)


def shards(volume, tissue, w_conv, gamma, beta, w_down, b_down):
    own_index = lax.axis_index("gx")
    size_x, size_y, merged = volume.shape
    size_z = merged // CIN
    tiles_x, tiles_y, tiles_z = size_x // TILE, size_y // TILE, size_z // TILE
    half = TILE // 2
    low_x, high_x, low_y, high_y = halo_pieces(volume)
    down = w_down.reshape(4, 2 * CMID, COUT)
    own_tissue = lax.dynamic_slice_in_dim(tissue, own_index * tiles_x, tiles_x, 0)
    flags = own_tissue.reshape(tiles_x * tiles_y * tiles_z).astype(jnp.int32)

    full = lambda shape: pl.BlockSpec(shape, lambda i, j, f: (0,) * len(shape))
    grid_spec = pltpu.PrefetchScalarGridSpec(
        num_scalar_prefetch=1,
        grid=(tiles_x, tiles_y),
        in_specs=[
            pl.BlockSpec(memory_space=pl.ANY),
            full(low_x.shape),
            full(high_x.shape),
            full(low_y.shape),
            full(high_y.shape),
            full((27, CIN, CMID)),
            full((1, CMID)),
            full((1, CMID)),
            full((4, 2 * CMID, COUT)),
            full((1, COUT)),
        ],
        out_specs=pl.BlockSpec((half, half, size_z // 2 * COUT), lambda i, j, f: (i, j, 0)),
        scratch_shapes=[
            pltpu.VMEM((size_x + 2, size_y + 2 * TILE, merged + 2 * CIN), jnp.bfloat16),
            pltpu.VMEM((TILE, TILE * TILE, CMID), jnp.float32),
            pltpu.VMEM((9, 4 * CIN, 2 * CMID), jnp.bfloat16),
            pltpu.VMEM((1, CMID), jnp.float32),
            pltpu.VMEM(volume.shape, jnp.bfloat16),
            pltpu.SemaphoreType.DMA((4,)),
        ],
    )
    return pl.pallas_call(
        tile_kernel,
        grid_spec=grid_spec,
        out_shape=jax.ShapeDtypeStruct((size_x // 2, size_y // 2, size_z // 2 * COUT),
                                       jnp.bfloat16),
    )(
        flags,
        volume,
        low_x,
        high_x,
        low_y,
        high_y,
        w_conv.reshape(27, CIN, CMID),
        gamma.reshape(1, CMID),
        beta.reshape(1, CMID),
        down,
        b_down.reshape(1, COUT),
    )


def solution(mesh):
    in_specs = (P("gx", "gy", None), P(None, "gy", None), P(), P(), P(), P(), P())
    out_specs = P("gx", "gy", None)
    return jax.shard_map(shards, mesh=mesh, in_specs=in_specs, out_specs=out_specs, check_vma=False)
```
